512 devices in a mesh: dp: 64 (over z_lo, y, core), seq: 8 (over x, z_hi).
Axes of the slice: x: 4, y: 8, z: 8 (z_hi: 2, z_lo: 4; z = z_hi * 4 + z_lo), core: 2. Of those that a mesh axis runs over, the one named last changes fastest.
Arguments:
- queries: bfloat16 [65536, 3072], P(('dp', 'seq'))
- keys: bfloat16 [65536, 1024], P(('dp', 'seq'))
- values: bfloat16 [65536, 1024], P(('dp', 'seq')), may hold values from -6 to 6
- output_gradient: bfloat16 [65536, 3072], P(('dp', 'seq')), may hold values from -48 to 48
- seg_lengths: int32 [64, 4], P('dp'), may hold values from 2 to 512, as said below
- knocked: int32 [64, 2], replicated, may hold values from 0 to 7, all different within a row
- source: int32 [64], replicated, may hold values from 0 to 63, as said below
Outputs:
- query_grad: bfloat16 [65536, 3072], P(('dp', 'seq'))
- key_grad: bfloat16 [65536, 1024], P(('dp', 'seq'))
- value_grad: bfloat16 [65536, 1024], P(('dp', 'seq'))
The draws below stay inside these ranges and needn't reach their ends.
Inputs may be any that keep to these rules, and one draw needn't show every extreme that they name: `knocked`: row p lists 2 different key-value heads of prompt p; every head is listed in some row. source is a permutation of the prompts with source[p] != p. `seg_lengths`: each row holds 4 even lengths that sum to 1024; one of them is exactly 512.
All inputs are finite; a program needn't handle non-finite values.
Results may differ from the reference program's by a relative error of at most 0.005.
Values may be sent and summed in bfloat16 or wider, within the bound.
No kernel may reach another device: no remote copies, remote signals or barrier semaphores. Data moves between devices by JAX's collectives and lax.ppermute only.
A program may use at most 64 MiB of HBM per device.

```python
import math
import jax
import jax.numpy as jnp
from jax import lax

QUERY_HEADS = 24
KEY_VALUE_HEADS = 8
HEAD_WIDTH = 128
KNOCKOUT_COUNT = 2
SEGS = 4
PROMPT_LENGTH = 1024
PROMPT_TOTAL = 64
TOKEN_TOTAL = 65536


def rough_rows(draw_key, complete_shape):
    return jnp.clip(jax.random.normal(jax.random.fold_in(draw_key, 1), complete_shape, jnp.float32), -6.0, 6.0)


def draw_queries(key, part):
    draw_key = jax.random.fold_in(key, 1)
    complete_shape = (PROMPT_TOTAL, PROMPT_LENGTH, QUERY_HEADS, HEAD_WIDTH)
    sample_draw = rough_rows(draw_key, complete_shape)
    return sample_draw.reshape(PROMPT_TOTAL * PROMPT_LENGTH, QUERY_HEADS * HEAD_WIDTH).astype(jnp.bfloat16)


def draw_keys(key, part):
    draw_key = jax.random.fold_in(key, 2)
    complete_shape = (PROMPT_TOTAL, PROMPT_LENGTH, KEY_VALUE_HEADS, HEAD_WIDTH)
    sample_draw = rough_rows(draw_key, complete_shape)
    return sample_draw.reshape(PROMPT_TOTAL * PROMPT_LENGTH, KEY_VALUE_HEADS * HEAD_WIDTH).astype(jnp.bfloat16)


def one_prompt(prompt_key):
    half_len = PROMPT_LENGTH // 2
    chosen = jax.random.permutation(jax.random.fold_in(prompt_key, 1), half_len // 2 - 1)[:SEGS - 2]
    boundaries = jnp.sort((chosen + 1) * 2).astype(jnp.int32)
    bounds = jnp.concatenate([jnp.zeros((1,), jnp.int32), boundaries, jnp.full((1,), half_len, jnp.int32)])
    others = bounds[1:] - bounds[:-1]
    big_slot = jax.random.randint(jax.random.fold_in(prompt_key, 2), (), 0, SEGS).astype(jnp.int32)
    slots = jnp.arange(SEGS, dtype=jnp.int32)
    other_index = jnp.clip(slots - (slots > big_slot).astype(jnp.int32), 0, SEGS - 2)
    return jnp.where(slots == big_slot, half_len, jnp.take(others, other_index)).astype(jnp.int32)


def draw_seg_lengths(key, part):
    prompt_keys = jax.random.split(jax.random.fold_in(key, 3), PROMPT_TOTAL)
    return jax.vmap(one_prompt)(prompt_keys).astype(jnp.int32)


def draw_source(key, part):
    ordering = jax.random.permutation(jax.random.fold_in(key, 4), PROMPT_TOTAL).astype(jnp.int32)
    return jnp.zeros((PROMPT_TOTAL,), jnp.int32).at[ordering].set(jnp.roll(ordering, -1))


def block_scale(rng, extent, shards, least, high):
    def one(dim, parts):
        draws = jax.random.uniform(jax.random.fold_in(jax.random.fold_in(rng, 6), dim), (parts,), jnp.float32, least / len(shards), high / len(shards))
        return jnp.repeat(jnp.exp(draws), extent[dim] // parts).reshape((-1,) + (1,) * (len(extent) - dim - 1))

    level = one(*shards[0])
    for cut in shards[1:]:
        level = level * one(*cut)
    return level


def distinct(own_key, rows, number_of, top, lift):
    sequence = jax.random.permutation(jax.random.fold_in(own_key, 1), number_of)
    pull = sequence
    for power in range(3):
        pull = pull * pull // number_of
    pull = pull * lift // number_of
    lots = jax.random.randint(jax.random.fold_in(own_key, 2), (rows, number_of), 0, 4096) + pull
    sure = jax.random.permutation(jax.random.fold_in(own_key, 3), rows)[jnp.arange(number_of) % rows]
    lots = jnp.where(jnp.arange(rows)[:, None] == sure[None, :], 1 << 14, lots)
    merit = lots * number_of + jnp.arange(number_of)
    return lax.top_k(merit.astype(jnp.int32), top)[1].astype(jnp.int32)


def centred(stream_key, extent, spread, bound, shards=(), kind=jnp.bfloat16):
    drawn = spread * jax.random.normal(stream_key, extent, jnp.float32)
    if shards:
        drawn = drawn * block_scale(stream_key, extent, shards, -0.22, 0.18)
    return jnp.clip(drawn, -bound, bound).astype(kind)


def setup_inputs(seed: int = 0) -> dict:
    key_list = jax.random.split(jax.random.key(seed), 8)
    queries = draw_queries(jax.random.fold_in(key_list[7], 71), 0)
    keys = draw_keys(jax.random.fold_in(key_list[7], 71), 0)
    values = centred(key_list[2], (TOKEN_TOTAL, KEY_VALUE_HEADS * HEAD_WIDTH), 1.0, 6.0, ((0, 512),))
    output_gradient = centred(key_list[3], (TOKEN_TOTAL, QUERY_HEADS * HEAD_WIDTH), 8.0, 48.0, ((0, 512),))
    seg_lengths = draw_seg_lengths(jax.random.fold_in(key_list[7], 71), 0)
    knocked = distinct(key_list[5], PROMPT_TOTAL, KEY_VALUE_HEADS, KNOCKOUT_COUNT, 0)
    source = draw_source(jax.random.fold_in(key_list[7], 71), 0)
    return {"queries": queries, "keys": keys, "values": values, "output_gradient": output_gradient, "seg_lengths": seg_lengths, "knocked": knocked, "source": source}


def document_mask(lengths, length):
    doc_ends = jnp.cumsum(lengths).astype(jnp.int32)
    position = jnp.arange(length, dtype=jnp.int32)
    segment = lax.optimization_barrier(jnp.sum((position[:, None] >= doc_ends[None, :]).astype(jnp.int32), axis=1))
    causal = position[:, None] >= position[None, :]
    return jnp.logical_and(causal, segment[:, None] == segment[None, :])

def head_backward(query_rows, key_rows, value_rows, grad_rows, visible):
    scaling = 1.0 / math.sqrt(HEAD_WIDTH)
    query_wide = query_rows.astype(jnp.float32)
    key_wide = key_rows.astype(jnp.float32)
    value_wide = value_rows.astype(jnp.float32)
    grad_wide = grad_rows.astype(jnp.float32)
    scores = jnp.einsum('id,jd->ij', query_wide, key_wide) * scaling
    scores = jnp.where(visible, scores, -jnp.inf)
    row_max = lax.optimization_barrier(jnp.max(scores, axis=1, keepdims=True))
    weights = jnp.exp(scores - row_max)
    attn_probs = weights / lax.optimization_barrier(jnp.sum(weights, axis=1, keepdims=True))
    probs_low = attn_probs.astype(jnp.bfloat16)
    value_part = jnp.einsum('ij,id->jd', probs_low.astype(jnp.float32), grad_wide)
    prob_grads = jnp.einsum('id,jd->ij', grad_wide, value_wide)
    row_delta = lax.optimization_barrier(jnp.sum(attn_probs * prob_grads, axis=1, keepdims=True))
    score_grads = (attn_probs * (prob_grads - row_delta) * scaling).astype(jnp.bfloat16)
    score_wide = score_grads.astype(jnp.float32)
    query_part = jnp.einsum('ij,jd->id', score_wide, key_wide).astype(jnp.bfloat16)
    key_part = jnp.einsum('ij,id->jd', score_wide, query_wide)
    return (query_part, key_part, value_part)

def prompt_backward(operands):
    heads_of_query, heads_of_key, heads_of_value, heads_gradient, lengths = operands
    visible = document_mask(lengths, PROMPT_LENGTH)

    def group_backward(group_operands):
        query_group, key_rows, value_rows, grad_group = group_operands

        def single_head(head_operands):
            return head_backward(head_operands[0], key_rows, value_rows, head_operands[1], visible)
        query_parts, key_parts, value_parts = lax.map(single_head, (query_group, grad_group))
        return (query_parts, lax.optimization_barrier(jnp.sum(key_parts, axis=0)), lax.optimization_barrier(jnp.sum(value_parts, axis=0)))
    return lax.map(group_backward, (heads_of_query, heads_of_key, heads_of_value, heads_gradient))

def reference(queries, keys, values, output_gradient, seg_lengths, knocked, source):
    group_width = QUERY_HEADS // KEY_VALUE_HEADS
    heads_of_query = queries.reshape(PROMPT_TOTAL, PROMPT_LENGTH, KEY_VALUE_HEADS, group_width, HEAD_WIDTH).transpose(0, 2, 3, 1, 4)
    heads_gradient = output_gradient.reshape(PROMPT_TOTAL, PROMPT_LENGTH, KEY_VALUE_HEADS, group_width, HEAD_WIDTH).transpose(0, 2, 3, 1, 4)
    heads_of_key = keys.reshape(PROMPT_TOTAL, PROMPT_LENGTH, KEY_VALUE_HEADS, HEAD_WIDTH).transpose(0, 2, 1, 3)
    heads_of_value = values.reshape(PROMPT_TOTAL, PROMPT_LENGTH, KEY_VALUE_HEADS, HEAD_WIDTH).transpose(0, 2, 1, 3)
    head_numbers = jnp.arange(KEY_VALUE_HEADS, dtype=jnp.int32)
    knocked_heads = jnp.any(knocked[:, :, None] == head_numbers[None, None, :], axis=1)
    used_keys = jnp.where(knocked_heads[:, :, None, None], heads_of_key[source], heads_of_key)
    query_grads, key_grads, value_gradient = lax.map(prompt_backward, (heads_of_query, used_keys, heads_of_value, heads_gradient, seg_lengths))
    own_part = jnp.where(knocked_heads[:, :, None, None], 0.0, key_grads)
    patched = jnp.zeros_like(key_grads).at[source].add(jnp.where(knocked_heads[:, :, None, None], key_grads, 0.0))
    key_overall = (own_part + patched).astype(jnp.bfloat16)
    query_out = query_grads.transpose(0, 3, 1, 2, 4).reshape(TOKEN_TOTAL, QUERY_HEADS * HEAD_WIDTH)
    key_result = key_overall.transpose(0, 2, 1, 3).reshape(TOKEN_TOTAL, KEY_VALUE_HEADS * HEAD_WIDTH)
    value_result = value_gradient.astype(jnp.bfloat16).transpose(0, 2, 1, 3).reshape(TOKEN_TOTAL, KEY_VALUE_HEADS * HEAD_WIDTH)
    return (query_out, key_result, value_result)
```

```python
import math

import jax
import jax.numpy as jnp
from jax import lax
from jax.sharding import PartitionSpec as P

KEY_VALUE_HEADS = 8
HEAD_WIDTH = 128
KNOCKOUT_COUNT = 2


masked_score = -1e30


def document_mask(lengths, length):
    doc_ends = jnp.cumsum(lengths)
    position = jnp.arange(length, dtype=jnp.int32)
    segment = jnp.sum((position[:, None] >= doc_ends[None, :]).astype(jnp.int32), axis=1)
    causal = position[:, None] >= position[None, :]
    return jnp.logical_and(causal, segment[:, None] == segment[None, :])


def attend_back(query_side, key_side, value_side, grad_side, visible):
    length = query_side.shape[0]
    heads_of_query = query_side.shape[1] // HEAD_WIDTH
    scaling = 1.0 / math.sqrt(HEAD_WIDTH)

    def one_head(head_index, totals):
        query_grads, key_grads, value_gradient = totals
        query_rows = lax.dynamic_slice_in_dim(query_side, head_index * HEAD_WIDTH, HEAD_WIDTH, 1)
        grad_rows = lax.dynamic_slice_in_dim(grad_side, head_index * HEAD_WIDTH, HEAD_WIDTH, 1)
        scores = (
            jnp.einsum("id,jd->ij", query_rows, key_side, preferred_element_type=jnp.float32)
            * scaling
        )
        scores = jnp.where(visible, scores, masked_score)
        row_max = jnp.max(scores, axis=1, keepdims=True)
        weights = jnp.exp(scores - row_max)
        attn_probs = weights / jnp.sum(weights, axis=1, keepdims=True)
        probs_low = attn_probs.astype(jnp.bfloat16)
        value_part = jnp.einsum(
            "ij,id->jd", probs_low, grad_rows, preferred_element_type=jnp.float32
        )
        prob_grads = jnp.einsum(
            "id,jd->ij", grad_rows, value_side, preferred_element_type=jnp.float32
        )
        row_delta = jnp.sum(attn_probs * prob_grads, axis=1, keepdims=True)
        score_grads = (attn_probs * (prob_grads - row_delta) * scaling).astype(jnp.bfloat16)
        query_part = jnp.dot(score_grads, key_side, preferred_element_type=jnp.float32)
        key_part = jnp.einsum(
            "ij,id->jd", score_grads, query_rows, preferred_element_type=jnp.float32
        )
        query_grads = lax.dynamic_update_slice_in_dim(
            query_grads, query_part.astype(jnp.bfloat16), head_index * HEAD_WIDTH, 1
        )
        key_grads = key_grads + key_part
        value_gradient = value_gradient + value_part
        return (query_grads, key_grads, value_gradient)

    initial = (
        jnp.zeros((length, query_side.shape[1]), jnp.bfloat16),
        jnp.zeros((length, key_side.shape[1]), jnp.float32),
        jnp.zeros((length, value_side.shape[1]), jnp.float32),
    )
    return lax.fori_loop(0, heads_of_query, one_head, initial)


def route(payload, order):
    prompt_count = lax.axis_size("dp")
    flat = payload.reshape(prompt_count, -1)
    spread = lax.all_to_all(flat, "dp", 0, 0, tiled=True)
    routed = jnp.take(spread, order, axis=0)
    back = lax.all_to_all(routed, "dp", 0, 0, tiled=True)
    return back.reshape(payload.shape)


def pick_heads(block, heads):
    parts = [
        lax.dynamic_slice_in_dim(block, heads[k] * HEAD_WIDTH, HEAD_WIDTH, 1)
        for k in range(KNOCKOUT_COUNT)
    ]
    return jnp.stack(parts, axis=1)


def per_device(queries, keys, values, output_gradient, seg_lengths, knocked, source):
    sequence_count = lax.axis_size("seq")
    prompt_count = lax.axis_size("dp")
    tok_rows = queries.shape[0]
    length = tok_rows * sequence_count
    prompt_index = lax.axis_index("dp")
    prompt_ids = jnp.arange(prompt_count, dtype=jnp.int32)
    consumer = jnp.sum(
        jnp.where(source[None, :] == prompt_ids[:, None], prompt_ids[None, :], 0), axis=1
    )
    my_knock = knocked[prompt_index]
    their_knock = knocked[consumer[prompt_index]]
    head_ids = jnp.arange(KEY_VALUE_HEADS, dtype=jnp.int32)[None, :, None]
    visible = document_mask(seg_lengths[0], length)

    outgoing = pick_heads(keys, their_knock)
    fetched = route(outgoing, source)
    keys3 = keys.reshape(tok_rows, KEY_VALUE_HEADS, HEAD_WIDTH)
    used3 = keys3
    for k in range(KNOCKOUT_COUNT - 1, -1, -1):
        used3 = jnp.where(head_ids == my_knock[k], fetched[:, k : k + 1, :], used3)
    used_keys = used3.reshape(tok_rows, -1)

    def cols(x):
        return x.reshape(tok_rows, sequence_count, -1)

    packed = jnp.concatenate(
        [cols(queries), cols(output_gradient), cols(used_keys), cols(values)], axis=2
    )
    widths = (
        queries.shape[1] // sequence_count,
        output_gradient.shape[1] // sequence_count,
        keys.shape[1] // sequence_count,
        values.shape[1] // sequence_count,
    )
    gathered = lax.all_to_all(packed, "seq", split_axis=1, concat_axis=0, tiled=True)
    gathered = gathered.reshape(length, -1)
    offsets = [0]
    for w in widths:
        offsets.append(offsets[-1] + w)
    query_side, grad_side, key_side, value_side = (
        gathered[:, offsets[i] : offsets[i + 1]] for i in range(4)
    )

    query_grads, key_grads, value_gradient = attend_back(
        query_side, key_side, value_side, grad_side, visible
    )

    low = jnp.concatenate([query_grads, value_gradient.astype(jnp.bfloat16)], axis=1)
    low_back = lax.all_to_all(low, "seq", split_axis=0, concat_axis=1, tiled=True)
    low_back = low_back.reshape(tok_rows, sequence_count, -1)
    query_out = low_back[:, :, : widths[0]].reshape(tok_rows, -1)
    value_out = low_back[:, :, widths[0] :].reshape(tok_rows, -1)
    key_back = lax.all_to_all(key_grads, "seq", split_axis=0, concat_axis=1, tiled=True)

    returning = pick_heads(key_back, my_knock)
    returned = route(returning, consumer)
    key3 = key_back.reshape(tok_rows, KEY_VALUE_HEADS, HEAD_WIDTH)
    own = key3
    for k in range(KNOCKOUT_COUNT):
        own = jnp.where(head_ids == my_knock[k], 0.0, own)
    extra = jnp.zeros_like(key3)
    for k in range(KNOCKOUT_COUNT):
        extra = jnp.where(head_ids == their_knock[k], returned[:, k : k + 1, :], extra)
    key_out = (own + extra).astype(jnp.bfloat16).reshape(tok_rows, -1)
    return (query_out, key_out, value_out)


def solution(mesh):
    placed = (
        P(("dp", "seq"), None),
        P(("dp", "seq"), None),
        P(("dp", "seq"), None),
        P(("dp", "seq"), None),
        P("dp", None),
        P(),
        P(),
    )
    return jax.shard_map(
        per_device,
        mesh=mesh,
        in_specs=placed,
        out_specs=(P(("dp", "seq"), None), P(("dp", "seq"), None), P(("dp", "seq"), None)),
        check_vma=False,
    )
```

```python
import math

import jax
import jax.numpy as jnp
from jax import lax
from jax.sharding import PartitionSpec as P

KEY_VALUE_HEADS = 8
HEAD_WIDTH = 128
KNOCKOUT_COUNT = 2


masked_score = -1e30


def document_mask(lengths, position):
    doc_ends = jnp.cumsum(lengths)
    segment = jnp.sum((position[:, None] >= doc_ends[None, :]).astype(jnp.int32), axis=1)
    causal = position[:, None] >= position[None, :]
    return jnp.logical_and(causal, segment[:, None] == segment[None, :])


def seq_send(blocks, axis, by_destination=True):
    count = lax.axis_size("seq")
    me = lax.axis_index("seq")
    received = []
    for k in range(count):
        index = me ^ k if by_destination else k
        part = lax.dynamic_index_in_dim(blocks, index, axis, keepdims=True)
        if k == 0:
            received.append(part)
            continue
        pairs = [(d, d ^ k) for d in range(count)]
        received.append(lax.ppermute(part, "seq", pairs))
    return jnp.concatenate(received, axis=axis)


def seq_place(received, axis):
    count = lax.axis_size("seq")
    me = lax.axis_index("seq")
    out = jnp.zeros_like(received)
    for k in range(count):
        part = lax.dynamic_index_in_dim(received, k, axis, keepdims=True)
        out = lax.dynamic_update_index_in_dim(out, part, me ^ k, axis)
    return out


def attend_back(query_side, key_side, value_side, grad_side, visible):
    length = query_side.shape[0]
    heads_of_query = query_side.shape[1] // HEAD_WIDTH
    scaling = 1.0 / math.sqrt(HEAD_WIDTH)

    def one_head(head_index, totals):
        query_grads, key_grads, value_gradient = totals
        query_rows = lax.dynamic_slice_in_dim(query_side, head_index * HEAD_WIDTH, HEAD_WIDTH, 1)
        grad_rows = lax.dynamic_slice_in_dim(grad_side, head_index * HEAD_WIDTH, HEAD_WIDTH, 1)
        scores = (
            jnp.einsum("id,jd->ij", query_rows, key_side, preferred_element_type=jnp.float32)
            * scaling
        )
        scores = jnp.where(visible, scores, masked_score)
        row_max = jnp.max(scores, axis=1, keepdims=True)
        weights = jnp.exp(scores - row_max)
        attn_probs = weights / jnp.sum(weights, axis=1, keepdims=True)
        probs_low = attn_probs.astype(jnp.bfloat16)
        value_part = jnp.einsum(
            "ij,id->jd", probs_low, grad_rows, preferred_element_type=jnp.float32
        )
        prob_grads = jnp.einsum(
            "id,jd->ij", grad_rows, value_side, preferred_element_type=jnp.float32
        )
        row_delta = jnp.sum(attn_probs * prob_grads, axis=1, keepdims=True)
        score_grads = (attn_probs * (prob_grads - row_delta) * scaling).astype(jnp.bfloat16)
        query_part = jnp.dot(score_grads, key_side, preferred_element_type=jnp.float32)
        key_part = jnp.einsum(
            "ij,id->jd", score_grads, query_rows, preferred_element_type=jnp.float32
        )
        query_grads = lax.dynamic_update_slice_in_dim(
            query_grads, query_part.astype(jnp.bfloat16), head_index * HEAD_WIDTH, 1
        )
        key_grads = key_grads + key_part
        value_gradient = value_gradient + value_part
        return (query_grads, key_grads, value_gradient)

    initial = (
        jnp.zeros((length, query_side.shape[1]), jnp.bfloat16),
        jnp.zeros((length, key_side.shape[1]), jnp.float32),
        jnp.zeros((length, value_side.shape[1]), jnp.float32),
    )
    return lax.fori_loop(0, heads_of_query, one_head, initial)


def route(payload, order):
    prompt_count = lax.axis_size("dp")
    flat = payload.reshape(prompt_count, -1)
    spread = lax.all_to_all(flat, "dp", 0, 0, tiled=True)
    routed = jnp.take(spread, order, axis=0)
    back = lax.all_to_all(routed, "dp", 0, 0, tiled=True)
    return back.reshape(payload.shape)


def pick_heads(block, heads):
    parts = [
        lax.dynamic_slice_in_dim(block, heads[k] * HEAD_WIDTH, HEAD_WIDTH, 1)
        for k in range(KNOCKOUT_COUNT)
    ]
    return jnp.stack(parts, axis=1)


def per_device(queries, keys, values, output_gradient, seg_lengths, knocked, source):
    sequence_count = lax.axis_size("seq")
    prompt_count = lax.axis_size("dp")
    tok_rows = queries.shape[0]
    length = tok_rows * sequence_count
    prompt_index = lax.axis_index("dp")
    prompt_ids = jnp.arange(prompt_count, dtype=jnp.int32)
    consumer = jnp.sum(
        jnp.where(source[None, :] == prompt_ids[:, None], prompt_ids[None, :], 0), axis=1
    )
    my_knock = knocked[prompt_index]
    their_knock = knocked[consumer[prompt_index]]
    head_ids = jnp.arange(KEY_VALUE_HEADS, dtype=jnp.int32)[None, :, None]

    outgoing = pick_heads(keys, their_knock)
    fetched = route(outgoing, source)
    keys3 = keys.reshape(tok_rows, KEY_VALUE_HEADS, HEAD_WIDTH)
    used3 = keys3
    for k in range(KNOCKOUT_COUNT - 1, -1, -1):
        used3 = jnp.where(head_ids == my_knock[k], fetched[:, k : k + 1, :], used3)
    used_keys = used3.reshape(tok_rows, -1)

    def cols(x):
        return x.reshape(tok_rows, sequence_count, -1)

    seq_index = lax.axis_index("seq")
    packed = jnp.concatenate([cols(queries), cols(output_gradient), cols(values)], axis=2)
    q_width = queries.shape[1] // sequence_count
    g_width = output_gradient.shape[1] // sequence_count
    gathered = seq_send(packed, 1)
    gathered = jnp.swapaxes(gathered, 0, 1).reshape(length, -1)
    query_side = gathered[:, :q_width]
    grad_side = gathered[:, q_width : q_width + g_width]
    value_side = gathered[:, q_width + g_width :]
    key_side = seq_send(cols(used_keys), 1)
    key_side = jnp.swapaxes(key_side, 0, 1).reshape(length, -1)

    rows = jnp.arange(length, dtype=jnp.int32)
    position = ((rows // tok_rows) ^ seq_index) * tok_rows + rows % tok_rows
    visible = document_mask(seg_lengths[0], position)

    query_grads, key_grads, value_gradient = attend_back(
        query_side, key_side, value_side, grad_side, visible
    )

    low = jnp.concatenate([query_grads, value_gradient.astype(jnp.bfloat16)], axis=1)
    low = low.reshape(sequence_count, tok_rows, -1)
    low_back = seq_place(seq_send(low, 0, False), 0)
    low_back = jnp.swapaxes(low_back, 0, 1)
    query_out = low_back[:, :, :q_width].reshape(tok_rows, -1)
    value_out = low_back[:, :, q_width:].reshape(tok_rows, -1)
    key_back = seq_place(seq_send(key_grads.reshape(sequence_count, tok_rows, -1), 0, False), 0)
    key_back = jnp.swapaxes(key_back, 0, 1).reshape(tok_rows, -1)

    returning = pick_heads(key_back, my_knock)
    returned = route(returning, consumer)
    key3 = key_back.reshape(tok_rows, KEY_VALUE_HEADS, HEAD_WIDTH)
    own = key3
    for k in range(KNOCKOUT_COUNT):
        own = jnp.where(head_ids == my_knock[k], 0.0, own)
    extra = jnp.zeros_like(key3)
    for k in range(KNOCKOUT_COUNT):
        extra = jnp.where(head_ids == their_knock[k], returned[:, k : k + 1, :], extra)
    key_out = (own + extra).astype(jnp.bfloat16).reshape(tok_rows, -1)
    return (query_out, key_out, value_out)


def solution(mesh):
    placed = (
        P(("dp", "seq"), None),
        P(("dp", "seq"), None),
        P(("dp", "seq"), None),
        P(("dp", "seq"), None),
        P("dp", None),
        P(),
        P(),
    )
    return jax.shard_map(
        per_device,
        mesh=mesh,
        in_specs=placed,
        out_specs=(P(("dp", "seq"), None), P(("dp", "seq"), None), P(("dp", "seq"), None)),
        check_vma=False,
    )
```

```python
import math

import jax
import jax.numpy as jnp
from jax import lax
from jax.sharding import PartitionSpec as P

KEY_VALUE_HEADS = 8
HEAD_WIDTH = 128
KNOCKOUT_COUNT = 2


masked_score = -1e30


def document_mask(lengths, length):
    doc_ends = jnp.cumsum(lengths)
    position = jnp.arange(length, dtype=jnp.int32)
    segment = jnp.sum((position[:, None] >= doc_ends[None, :]).astype(jnp.int32), axis=1)
    causal = position[:, None] >= position[None, :]
    return jnp.logical_and(causal, segment[:, None] == segment[None, :])


def attend_back(query_side, key_side, value_side, grad_side, visible):
    length = query_side.shape[0]
    heads_of_query = query_side.shape[1] // HEAD_WIDTH
    scaling = 1.0 / math.sqrt(HEAD_WIDTH)

    def one_head(head_index, totals):
        query_grads, key_grads, value_gradient = totals
        query_rows = lax.dynamic_slice_in_dim(query_side, head_index * HEAD_WIDTH, HEAD_WIDTH, 1)
        grad_rows = lax.dynamic_slice_in_dim(grad_side, head_index * HEAD_WIDTH, HEAD_WIDTH, 1)
        scores = (
            jnp.einsum("id,jd->ij", query_rows, key_side, preferred_element_type=jnp.float32)
            * scaling
        )
        scores = jnp.where(visible, scores, masked_score)
        row_max = jnp.max(scores, axis=1, keepdims=True)
        weights = jnp.exp(scores - row_max)
        attn_probs = weights / jnp.sum(weights, axis=1, keepdims=True)
        probs_low = attn_probs.astype(jnp.bfloat16)
        value_part = jnp.einsum(
            "ij,id->jd", probs_low, grad_rows, preferred_element_type=jnp.float32
        )
        prob_grads = jnp.einsum(
            "id,jd->ij", grad_rows, value_side, preferred_element_type=jnp.float32
        )
        row_delta = jnp.sum(attn_probs * prob_grads, axis=1, keepdims=True)
        score_grads = (attn_probs * (prob_grads - row_delta) * scaling).astype(jnp.bfloat16)
        query_part = jnp.dot(score_grads, key_side, preferred_element_type=jnp.float32)
        key_part = jnp.einsum(
            "ij,id->jd", score_grads, query_rows, preferred_element_type=jnp.float32
        )
        query_grads = lax.dynamic_update_slice_in_dim(
            query_grads, query_part.astype(jnp.bfloat16), head_index * HEAD_WIDTH, 1
        )
        key_grads = key_grads + key_part
        value_gradient = value_gradient + value_part
        return (query_grads, key_grads, value_gradient)

    initial = (
        jnp.zeros((length, query_side.shape[1]), jnp.bfloat16),
        jnp.zeros((length, key_side.shape[1]), jnp.float32),
        jnp.zeros((length, value_side.shape[1]), jnp.float32),
    )
    return lax.fori_loop(0, heads_of_query, one_head, initial)


def route(payload, order):
    prompt_count = lax.axis_size("dp")
    flat = payload.reshape(prompt_count, -1)
    spread = lax.all_to_all(flat, "dp", 0, 0, tiled=True)
    routed = jnp.take(spread, order, axis=0)
    back = lax.all_to_all(routed, "dp", 0, 0, tiled=True)
    return back.reshape(payload.shape)


def pick_heads(block, heads):
    parts = [
        lax.dynamic_slice_in_dim(block, heads[k] * HEAD_WIDTH, HEAD_WIDTH, 1)
        for k in range(KNOCKOUT_COUNT)
    ]
    return jnp.stack(parts, axis=1)


def per_device(queries, keys, values, output_gradient, seg_lengths, knocked, source):
    sequence_count = lax.axis_size("seq")
    prompt_count = lax.axis_size("dp")
    tok_rows = queries.shape[0]
    length = tok_rows * sequence_count
    prompt_index = lax.axis_index("dp")
    prompt_ids = jnp.arange(prompt_count, dtype=jnp.int32)
    consumer = jnp.sum(
        jnp.where(source[None, :] == prompt_ids[:, None], prompt_ids[None, :], 0), axis=1
    )
    my_knock = knocked[prompt_index]
    their_knock = knocked[consumer[prompt_index]]
    head_ids = jnp.arange(KEY_VALUE_HEADS, dtype=jnp.int32)[None, :, None]
    visible = document_mask(seg_lengths[0], length)

    outgoing = pick_heads(keys, their_knock)
    fetched = route(outgoing, source)
    keys3 = keys.reshape(tok_rows, KEY_VALUE_HEADS, HEAD_WIDTH)
    used3 = keys3
    for k in range(KNOCKOUT_COUNT - 1, -1, -1):
        used3 = jnp.where(head_ids == my_knock[k], fetched[:, k : k + 1, :], used3)
    used_keys = used3.reshape(tok_rows, -1)

    def cols(x):
        return x.reshape(tok_rows, sequence_count, -1)

    packed = jnp.concatenate(
        [cols(queries), cols(output_gradient), cols(used_keys), cols(values)], axis=2
    )
    widths = (
        queries.shape[1] // sequence_count,
        output_gradient.shape[1] // sequence_count,
        keys.shape[1] // sequence_count,
        values.shape[1] // sequence_count,
    )
    gathered = lax.all_to_all(packed, "seq", split_axis=1, concat_axis=0, tiled=True)
    gathered = gathered.reshape(length, -1)
    offsets = [0]
    for w in widths:
        offsets.append(offsets[-1] + w)
    query_side, grad_side, key_side, value_side = (
        gathered[:, offsets[i] : offsets[i + 1]] for i in range(4)
    )

    query_grads, key_grads, value_gradient = attend_back(
        query_side, key_side, value_side, grad_side, visible
    )

    low = jnp.concatenate(
        [query_grads, value_gradient.astype(jnp.bfloat16), key_grads.astype(jnp.bfloat16)], axis=1
    )
    low_back = lax.all_to_all(low, "seq", split_axis=0, concat_axis=1, tiled=True)
    low_back = low_back.reshape(tok_rows, sequence_count, -1)
    v_end = widths[0] + widths[3]
    query_out = low_back[:, :, : widths[0]].reshape(tok_rows, -1)
    value_out = low_back[:, :, widths[0] : v_end].reshape(tok_rows, -1)
    key_back = low_back[:, :, v_end:].reshape(tok_rows, -1)

    returning = pick_heads(key_back, my_knock)
    returned = route(returning, consumer)
    key3 = key_back.reshape(tok_rows, KEY_VALUE_HEADS, HEAD_WIDTH)
    own = key3
    for k in range(KNOCKOUT_COUNT):
        own = jnp.where(head_ids == my_knock[k], jnp.zeros_like(own), own)
    extra = jnp.zeros_like(key3)
    for k in range(KNOCKOUT_COUNT):
        extra = jnp.where(head_ids == their_knock[k], returned[:, k : k + 1, :], extra)
    key_out = (own.astype(jnp.float32) + extra.astype(jnp.float32)).astype(jnp.bfloat16).reshape(tok_rows, -1)
    return (query_out, key_out, value_out)


def solution(mesh):
    placed = (
        P(("dp", "seq"), None),
        P(("dp", "seq"), None),
        P(("dp", "seq"), None),
        P(("dp", "seq"), None),
        P("dp", None),
        P(),
        P(),
    )
    return jax.shard_map(
        per_device,
        mesh=mesh,
        in_specs=placed,
        out_specs=(P(("dp", "seq"), None), P(("dp", "seq"), None), P(("dp", "seq"), None)),
        check_vma=False,
    )
```

```python
import math

import jax
import jax.numpy as jnp
from jax import lax
from jax.experimental import pallas as pl
from jax.experimental.pallas import tpu as pltpu
from jax.sharding import PartitionSpec as P

KEY_VALUE_HEADS = 8
HEAD_WIDTH = 128
KNOCKOUT_COUNT = 2


masked_score = -1e30


def document_mask(lengths, length):
    doc_ends = jnp.cumsum(lengths)
    position = jnp.arange(length, dtype=jnp.int32)
    segment = jnp.sum((position[:, None] >= doc_ends[None, :]).astype(jnp.int32), axis=1)
    causal = position[:, None] >= position[None, :]
    return jnp.logical_and(causal, segment[:, None] == segment[None, :])


def attend_back(query_side, key_side, value_side, grad_side, visible):
    length = query_side.shape[0]
    heads_of_query = query_side.shape[1] // HEAD_WIDTH
    scaling = 1.0 / math.sqrt(HEAD_WIDTH)

    def one_head(head_index, totals):
        query_grads, key_grads, value_gradient = totals
        query_rows = lax.dynamic_slice_in_dim(query_side, head_index * HEAD_WIDTH, HEAD_WIDTH, 1)
        grad_rows = lax.dynamic_slice_in_dim(grad_side, head_index * HEAD_WIDTH, HEAD_WIDTH, 1)
        scores = (
            jnp.einsum("id,jd->ij", query_rows, key_side, preferred_element_type=jnp.float32)
            * scaling
        )
        scores = jnp.where(visible, scores, masked_score)
        row_max = jnp.max(scores, axis=1, keepdims=True)
        weights = jnp.exp(scores - row_max)
        attn_probs = weights / jnp.sum(weights, axis=1, keepdims=True)
        probs_low = attn_probs.astype(jnp.bfloat16)
        value_part = jnp.einsum(
            "ij,id->jd", probs_low, grad_rows, preferred_element_type=jnp.float32
        )
        prob_grads = jnp.einsum(
            "id,jd->ij", grad_rows, value_side, preferred_element_type=jnp.float32
        )
        row_delta = jnp.sum(attn_probs * prob_grads, axis=1, keepdims=True)
        score_grads = (attn_probs * (prob_grads - row_delta) * scaling).astype(jnp.bfloat16)
        query_part = jnp.dot(score_grads, key_side, preferred_element_type=jnp.float32)
        key_part = jnp.einsum(
            "ij,id->jd", score_grads, query_rows, preferred_element_type=jnp.float32
        )
        query_grads = lax.dynamic_update_slice_in_dim(
            query_grads, query_part.astype(jnp.bfloat16), head_index * HEAD_WIDTH, 1
        )
        key_grads = key_grads + key_part
        value_gradient = value_gradient + value_part
        return (query_grads, key_grads, value_gradient)

    initial = (
        jnp.zeros((length, query_side.shape[1]), jnp.bfloat16),
        jnp.zeros((length, key_side.shape[1]), jnp.float32),
        jnp.zeros((length, value_side.shape[1]), jnp.float32),
    )
    return lax.fori_loop(0, heads_of_query, one_head, initial)


BLOCK_ROWS = 256


def attend_kernel(seg_row_ref, seg_col_ref, q_ref, g_ref, k_ref, v_ref, dq_ref, dk_ref, dv_ref):
    scaling = 1.0 / math.sqrt(HEAD_WIDTH)
    length = q_ref.shape[0]

    @pl.when(pl.program_id(0) == 0)
    def _():
        dk_ref[...] = jnp.zeros_like(dk_ref)
        dv_ref[...] = jnp.zeros_like(dv_ref)

    for block in range(length // BLOCK_ROWS):
        rows = pl.ds(block * BLOCK_ROWS, BLOCK_ROWS)
        span = (block + 1) * BLOCK_ROWS
        keys = k_ref[0:span, :]
        vals = v_ref[0:span, :]
        q_rows = q_ref[rows, :]
        g_rows = g_ref[rows, :]
        scores = lax.dot_general(
            q_rows, keys, (((1,), (1,)), ((), ())), preferred_element_type=jnp.float32
        ) * scaling
        row_pos = block * BLOCK_ROWS + lax.broadcasted_iota(jnp.int32, (BLOCK_ROWS, span), 0)
        col_pos = lax.broadcasted_iota(jnp.int32, (BLOCK_ROWS, span), 1)
        same = seg_row_ref[rows, :] == seg_col_ref[:, 0:span]
        visible = jnp.logical_and(row_pos >= col_pos, same)
        scores = jnp.where(visible, scores, masked_score)
        row_max = jnp.max(scores, axis=1, keepdims=True)
        weights = jnp.exp(scores - row_max)
        probs = weights / jnp.sum(weights, axis=1, keepdims=True)
        probs_low = probs.astype(jnp.bfloat16)
        dv_ref[0:span, :] += lax.dot_general(
            probs_low, g_rows, (((0,), (0,)), ((), ())), preferred_element_type=jnp.float32
        )
        prob_grads = lax.dot_general(
            g_rows, vals, (((1,), (1,)), ((), ())), preferred_element_type=jnp.float32
        )
        row_delta = jnp.sum(probs * prob_grads, axis=1, keepdims=True)
        score_grads = (probs * (prob_grads - row_delta) * scaling).astype(jnp.bfloat16)
        dq_ref[rows, :] = jnp.dot(
            score_grads, keys, preferred_element_type=jnp.float32
        ).astype(dq_ref.dtype)
        dk_ref[0:span, :] += lax.dot_general(
            score_grads, q_rows, (((0,), (0,)), ((), ())), preferred_element_type=jnp.float32
        )


def attend_back_kernel(gathered, segment, heads_of_query, q_block, g_block, k_block, v_block):
    length = gathered.shape[0]
    seg_row = segment.reshape(length, 1)
    seg_col = segment.reshape(1, length)
    full = lambda h: (0, 0)
    col = lambda b: pl.BlockSpec((length, HEAD_WIDTH), lambda h: (0, b))
    flops = 5 * 2 * length * length * HEAD_WIDTH * heads_of_query * 10 // 16
    return pl.pallas_call(
        attend_kernel,
        grid=(heads_of_query,),
        in_specs=[
            pl.BlockSpec((length, 1), full),
            pl.BlockSpec((1, length), full),
            pl.BlockSpec((length, HEAD_WIDTH), lambda h: (0, q_block + h)),
            pl.BlockSpec((length, HEAD_WIDTH), lambda h: (0, g_block + h)),
            col(k_block),
            col(v_block),
        ],
        out_specs=[
            pl.BlockSpec((length, HEAD_WIDTH), lambda h: (0, h)),
            pl.BlockSpec((length, HEAD_WIDTH), full),
            pl.BlockSpec((length, HEAD_WIDTH), full),
        ],
        out_shape=[
            jax.ShapeDtypeStruct((length, heads_of_query * HEAD_WIDTH), jnp.bfloat16),
            jax.ShapeDtypeStruct((length, HEAD_WIDTH), jnp.float32),
            jax.ShapeDtypeStruct((length, HEAD_WIDTH), jnp.float32),
        ],
        compiler_params=pltpu.CompilerParams(
            dimension_semantics=("arbitrary",), vmem_limit_bytes=48 * 1024 * 1024
        ),
        cost_estimate=pl.CostEstimate(
            flops=flops,
            transcendentals=length * length * heads_of_query * 10 // 16,
            bytes_accessed=length * HEAD_WIDTH * (2 * 2 * heads_of_query + 2 * 2 + 2 * heads_of_query + 8),
        ),
    )(seg_row, seg_col, gathered, gathered, gathered, gathered)


def route(payload, order):
    prompt_count = lax.axis_size("dp")
    flat = payload.reshape(prompt_count, -1)
    spread = lax.all_to_all(flat, "dp", 0, 0, tiled=True)
    routed = jnp.take(spread, order, axis=0)
    back = lax.all_to_all(routed, "dp", 0, 0, tiled=True)
    return back.reshape(payload.shape)


def pick_heads(block, heads):
    parts = [
        lax.dynamic_slice_in_dim(block, heads[k] * HEAD_WIDTH, HEAD_WIDTH, 1)
        for k in range(KNOCKOUT_COUNT)
    ]
    return jnp.stack(parts, axis=1)


def per_device(queries, keys, values, output_gradient, seg_lengths, knocked, source):
    sequence_count = lax.axis_size("seq")
    prompt_count = lax.axis_size("dp")
    tok_rows = queries.shape[0]
    length = tok_rows * sequence_count
    prompt_index = lax.axis_index("dp")
    prompt_ids = jnp.arange(prompt_count, dtype=jnp.int32)
    consumer = jnp.sum(
        jnp.where(source[None, :] == prompt_ids[:, None], prompt_ids[None, :], 0), axis=1
    )
    my_knock = knocked[prompt_index]
    their_knock = knocked[consumer[prompt_index]]
    head_ids = jnp.arange(KEY_VALUE_HEADS, dtype=jnp.int32)[None, :, None]

    outgoing = pick_heads(keys, their_knock)
    fetched = route(outgoing, source)
    keys3 = keys.reshape(tok_rows, KEY_VALUE_HEADS, HEAD_WIDTH)
    used3 = keys3
    for k in range(KNOCKOUT_COUNT - 1, -1, -1):
        used3 = jnp.where(head_ids == my_knock[k], fetched[:, k : k + 1, :], used3)
    used_keys = used3.reshape(tok_rows, -1)

    def cols(x):
        return x.reshape(tok_rows, sequence_count, -1)

    packed = jnp.concatenate(
        [cols(queries), cols(output_gradient), cols(used_keys), cols(values)], axis=2
    )
    widths = (
        queries.shape[1] // sequence_count,
        output_gradient.shape[1] // sequence_count,
        keys.shape[1] // sequence_count,
        values.shape[1] // sequence_count,
    )
    gathered = lax.all_to_all(packed, "seq", split_axis=1, concat_axis=0, tiled=True)
    gathered = gathered.reshape(length, -1)
    offsets = [0]
    for w in widths:
        offsets.append(offsets[-1] + w)

    doc_ends = jnp.cumsum(seg_lengths[0])
    position = jnp.arange(length, dtype=jnp.int32)
    segment = jnp.sum((position[:, None] >= doc_ends[None, :]).astype(jnp.int32), axis=1)
    heads_here = widths[0] // HEAD_WIDTH
    query_grads, key_grads, value_gradient = attend_back_kernel(
        gathered, segment, heads_here, 0, heads_here, 2 * heads_here, 2 * heads_here + 1
    )

    low = jnp.concatenate(
        [query_grads, value_gradient.astype(jnp.bfloat16), key_grads.astype(jnp.bfloat16)], axis=1
    )
    low_back = lax.all_to_all(low, "seq", split_axis=0, concat_axis=1, tiled=True)
    low_back = low_back.reshape(tok_rows, sequence_count, -1)
    v_end = widths[0] + widths[3]
    query_out = low_back[:, :, : widths[0]].reshape(tok_rows, -1)
    value_out = low_back[:, :, widths[0] : v_end].reshape(tok_rows, -1)
    key_back = low_back[:, :, v_end:].reshape(tok_rows, -1)

    returning = pick_heads(key_back, my_knock)
    returned = route(returning, consumer)
    key3 = key_back.reshape(tok_rows, KEY_VALUE_HEADS, HEAD_WIDTH)
    own = key3
    for k in range(KNOCKOUT_COUNT):
        own = jnp.where(head_ids == my_knock[k], jnp.zeros_like(own), own)
    extra = jnp.zeros_like(key3)
    for k in range(KNOCKOUT_COUNT):
        extra = jnp.where(head_ids == their_knock[k], returned[:, k : k + 1, :], extra)
    key_out = (own.astype(jnp.float32) + extra.astype(jnp.float32)).astype(jnp.bfloat16).reshape(tok_rows, -1)
    return (query_out, key_out, value_out)


def solution(mesh):
    placed = (
        P(("dp", "seq"), None),
        P(("dp", "seq"), None),
        P(("dp", "seq"), None),
        P(("dp", "seq"), None),
        P("dp", None),
        P(),
        P(),
    )
    return jax.shard_map(
        per_device,
        mesh=mesh,
        in_specs=placed,
        out_specs=(P(("dp", "seq"), None), P(("dp", "seq"), None), P(("dp", "seq"), None)),
        check_vma=False,
    )
```

```python
import math

import jax
import jax.numpy as jnp
from jax import lax
from jax.experimental import pallas as pl
from jax.experimental.pallas import tpu as pltpu
from jax.sharding import PartitionSpec as P

KEY_VALUE_HEADS = 8
HEAD_WIDTH = 128
KNOCKOUT_COUNT = 2


masked_score = -1e30


def document_mask(lengths, length):
    doc_ends = jnp.cumsum(lengths)
    position = jnp.arange(length, dtype=jnp.int32)
    segment = jnp.sum((position[:, None] >= doc_ends[None, :]).astype(jnp.int32), axis=1)
    causal = position[:, None] >= position[None, :]
    return jnp.logical_and(causal, segment[:, None] == segment[None, :])


def attend_back(query_side, key_side, value_side, grad_side, visible):
    length = query_side.shape[0]
    heads_of_query = query_side.shape[1] // HEAD_WIDTH
    scaling = 1.0 / math.sqrt(HEAD_WIDTH)

    def one_head(head_index, totals):
        query_grads, key_grads, value_gradient = totals
        query_rows = lax.dynamic_slice_in_dim(query_side, head_index * HEAD_WIDTH, HEAD_WIDTH, 1)
        grad_rows = lax.dynamic_slice_in_dim(grad_side, head_index * HEAD_WIDTH, HEAD_WIDTH, 1)
        scores = (
            jnp.einsum("id,jd->ij", query_rows, key_side, preferred_element_type=jnp.float32)
            * scaling
        )
        scores = jnp.where(visible, scores, masked_score)
        row_max = jnp.max(scores, axis=1, keepdims=True)
        weights = jnp.exp(scores - row_max)
        attn_probs = weights / jnp.sum(weights, axis=1, keepdims=True)
        probs_low = attn_probs.astype(jnp.bfloat16)
        value_part = jnp.einsum(
            "ij,id->jd", probs_low, grad_rows, preferred_element_type=jnp.float32
        )
        prob_grads = jnp.einsum(
            "id,jd->ij", grad_rows, value_side, preferred_element_type=jnp.float32
        )
        row_delta = jnp.sum(attn_probs * prob_grads, axis=1, keepdims=True)
        score_grads = (attn_probs * (prob_grads - row_delta) * scaling).astype(jnp.bfloat16)
        query_part = jnp.dot(score_grads, key_side, preferred_element_type=jnp.float32)
        key_part = jnp.einsum(
            "ij,id->jd", score_grads, query_rows, preferred_element_type=jnp.float32
        )
        query_grads = lax.dynamic_update_slice_in_dim(
            query_grads, query_part.astype(jnp.bfloat16), head_index * HEAD_WIDTH, 1
        )
        key_grads = key_grads + key_part
        value_gradient = value_gradient + value_part
        return (query_grads, key_grads, value_gradient)

    initial = (
        jnp.zeros((length, query_side.shape[1]), jnp.bfloat16),
        jnp.zeros((length, key_side.shape[1]), jnp.float32),
        jnp.zeros((length, value_side.shape[1]), jnp.float32),
    )
    return lax.fori_loop(0, heads_of_query, one_head, initial)


BLOCK_ROWS = 256


def attend_kernel(seg_row_ref, seg_col_ref, q_ref, g_ref, k_ref, v_ref, dq_ref, dk_ref, dv_ref):
    scaling = 1.0 / math.sqrt(HEAD_WIDTH)
    length = q_ref.shape[0]

    @pl.when(pl.program_id(0) == 0)
    def _():
        dk_ref[...] = jnp.zeros_like(dk_ref)
        dv_ref[...] = jnp.zeros_like(dv_ref)

    for block in range(length // BLOCK_ROWS):
        rows = pl.ds(block * BLOCK_ROWS, BLOCK_ROWS)
        span = (block + 1) * BLOCK_ROWS
        keys = k_ref[0:span, :]
        vals = v_ref[0:span, :]
        q_rows = q_ref[rows, :]
        g_rows = g_ref[rows, :]
        scores = lax.dot_general(
            q_rows, keys, (((1,), (1,)), ((), ())), preferred_element_type=jnp.float32
        ) * scaling
        row_pos = block * BLOCK_ROWS + lax.broadcasted_iota(jnp.int32, (BLOCK_ROWS, span), 0)
        col_pos = lax.broadcasted_iota(jnp.int32, (BLOCK_ROWS, span), 1)
        same = seg_row_ref[rows, :] == seg_col_ref[:, 0:span]
        visible = jnp.logical_and(row_pos >= col_pos, same)
        scores = jnp.where(visible, scores, masked_score)
        row_max = jnp.max(scores, axis=1, keepdims=True)
        weights = jnp.exp(scores - row_max)
        probs = weights / jnp.sum(weights, axis=1, keepdims=True)
        probs_low = probs.astype(jnp.bfloat16)
        dv_ref[0:span, :] += lax.dot_general(
            probs_low, g_rows, (((0,), (0,)), ((), ())), preferred_element_type=jnp.float32
        )
        prob_grads = lax.dot_general(
            g_rows, vals, (((1,), (1,)), ((), ())), preferred_element_type=jnp.float32
        )
        row_delta = jnp.sum(probs * prob_grads, axis=1, keepdims=True)
        score_grads = (probs * (prob_grads - row_delta) * scaling).astype(jnp.bfloat16)
        dq_ref[rows, :] = jnp.dot(
            score_grads, keys, preferred_element_type=jnp.float32
        ).astype(dq_ref.dtype)
        dk_ref[0:span, :] += lax.dot_general(
            score_grads, q_rows, (((0,), (0,)), ((), ())), preferred_element_type=jnp.float32
        )


def attend_back_kernel(gathered, segment, heads_of_query, q_block, g_block, k_block, v_block):
    length = gathered.shape[0]
    seg_row = segment.reshape(length, 1)
    seg_col = segment.reshape(1, length)
    full = lambda h: (0, 0)
    col = lambda b: pl.BlockSpec((length, HEAD_WIDTH), lambda h: (0, b))
    flops = 5 * 2 * length * length * HEAD_WIDTH * heads_of_query * 10 // 16
    return pl.pallas_call(
        attend_kernel,
        grid=(heads_of_query,),
        in_specs=[
            pl.BlockSpec((length, 1), full),
            pl.BlockSpec((1, length), full),
            pl.BlockSpec((length, HEAD_WIDTH), lambda h: (0, q_block + h)),
            pl.BlockSpec((length, HEAD_WIDTH), lambda h: (0, g_block + h)),
            col(k_block),
            col(v_block),
        ],
        out_specs=[
            pl.BlockSpec((length, HEAD_WIDTH), lambda h: (0, h)),
            pl.BlockSpec((length, HEAD_WIDTH), full),
            pl.BlockSpec((length, HEAD_WIDTH), full),
        ],
        out_shape=[
            jax.ShapeDtypeStruct((length, heads_of_query * HEAD_WIDTH), jnp.bfloat16),
            jax.ShapeDtypeStruct((length, HEAD_WIDTH), jnp.float32),
            jax.ShapeDtypeStruct((length, HEAD_WIDTH), jnp.float32),
        ],
        compiler_params=pltpu.CompilerParams(
            dimension_semantics=("arbitrary",), vmem_limit_bytes=48 * 1024 * 1024
        ),
        cost_estimate=pl.CostEstimate(
            flops=flops,
            transcendentals=length * length * heads_of_query * 10 // 16,
            bytes_accessed=length * HEAD_WIDTH * (2 * 2 * heads_of_query + 2 * 2 + 2 * heads_of_query + 8),
        ),
    )(seg_row, seg_col, gathered, gathered, gathered, gathered)


def route(block, order, heads):
    prompt_count = lax.axis_size("dp")
    rows = block.shape[0]
    flat = block.reshape(prompt_count, rows // prompt_count, KEY_VALUE_HEADS, HEAD_WIDTH)
    spread = lax.all_to_all(flat, "dp", 0, 0, tiled=True)
    routed = jnp.take(spread, order, axis=0)
    routed = jnp.take_along_axis(routed, heads[:, None, :, None], axis=2)
    back = lax.all_to_all(routed, "dp", 0, 0, tiled=True)
    return back.reshape(rows, KNOCKOUT_COUNT, HEAD_WIDTH)


def per_device(queries, keys, values, output_gradient, seg_lengths, knocked, source):
    sequence_count = lax.axis_size("seq")
    prompt_count = lax.axis_size("dp")
    tok_rows = queries.shape[0]
    length = tok_rows * sequence_count
    prompt_index = lax.axis_index("dp")
    prompt_ids = jnp.arange(prompt_count, dtype=jnp.int32)
    consumer = jnp.sum(
        jnp.where(source[None, :] == prompt_ids[:, None], prompt_ids[None, :], 0), axis=1
    )
    my_knock = knocked[prompt_index]
    their_knock = knocked[consumer[prompt_index]]
    head_ids = jnp.arange(KEY_VALUE_HEADS, dtype=jnp.int32)[None, :, None]

    fetched = route(keys, source, knocked)
    keys3 = keys.reshape(tok_rows, KEY_VALUE_HEADS, HEAD_WIDTH)
    used3 = keys3
    for k in range(KNOCKOUT_COUNT - 1, -1, -1):
        used3 = jnp.where(head_ids == my_knock[k], fetched[:, k : k + 1, :], used3)
    used_keys = used3.reshape(tok_rows, -1)

    def cols(x):
        return x.reshape(tok_rows, sequence_count, -1)

    packed = jnp.concatenate(
        [cols(queries), cols(output_gradient), cols(used_keys), cols(values)], axis=2
    )
    widths = (
        queries.shape[1] // sequence_count,
        output_gradient.shape[1] // sequence_count,
        keys.shape[1] // sequence_count,
        values.shape[1] // sequence_count,
    )
    gathered = lax.all_to_all(packed, "seq", split_axis=1, concat_axis=0, tiled=True)
    gathered = gathered.reshape(length, -1)
    offsets = [0]
    for w in widths:
        offsets.append(offsets[-1] + w)

    doc_ends = jnp.cumsum(seg_lengths[0])
    position = jnp.arange(length, dtype=jnp.int32)
    segment = jnp.sum((position[:, None] >= doc_ends[None, :]).astype(jnp.int32), axis=1)
    heads_here = widths[0] // HEAD_WIDTH
    query_grads, key_grads, value_gradient = attend_back_kernel(
        gathered, segment, heads_here, 0, heads_here, 2 * heads_here, 2 * heads_here + 1
    )

    low = jnp.concatenate(
        [query_grads, value_gradient.astype(jnp.bfloat16), key_grads.astype(jnp.bfloat16)], axis=1
    )
    low_back = lax.all_to_all(low, "seq", split_axis=0, concat_axis=1, tiled=True)
    low_back = low_back.reshape(tok_rows, sequence_count, -1)
    v_end = widths[0] + widths[3]
    query_out = low_back[:, :, : widths[0]].reshape(tok_rows, -1)
    value_out = low_back[:, :, widths[0] : v_end].reshape(tok_rows, -1)
    key_back = low_back[:, :, v_end:].reshape(tok_rows, -1)

    returned = route(key_back, consumer, knocked[consumer])
    key3 = key_back.reshape(tok_rows, KEY_VALUE_HEADS, HEAD_WIDTH)
    own = key3
    for k in range(KNOCKOUT_COUNT):
        own = jnp.where(head_ids == my_knock[k], jnp.zeros_like(own), own)
    extra = jnp.zeros_like(key3)
    for k in range(KNOCKOUT_COUNT):
        extra = jnp.where(head_ids == their_knock[k], returned[:, k : k + 1, :], extra)
    key_out = (own.astype(jnp.float32) + extra.astype(jnp.float32)).astype(jnp.bfloat16).reshape(tok_rows, -1)
    return (query_out, key_out, value_out)


def solution(mesh):
    placed = (
        P(("dp", "seq"), None),
        P(("dp", "seq"), None),
        P(("dp", "seq"), None),
        P(("dp", "seq"), None),
        P("dp", None),
        P(),
        P(),
    )
    return jax.shard_map(
        per_device,
        mesh=mesh,
        in_specs=placed,
        out_specs=(P(("dp", "seq"), None), P(("dp", "seq"), None), P(("dp", "seq"), None)),
        check_vma=False,
    )
```

```python
import math

import jax
import jax.numpy as jnp
from jax import lax
from jax.experimental import pallas as pl
from jax.experimental.pallas import tpu as pltpu
from jax.sharding import PartitionSpec as P

KEY_VALUE_HEADS = 8
HEAD_WIDTH = 128
KNOCKOUT_COUNT = 2


masked_score = -1e30


def document_mask(lengths, length):
    doc_ends = jnp.cumsum(lengths)
    position = jnp.arange(length, dtype=jnp.int32)
    segment = jnp.sum((position[:, None] >= doc_ends[None, :]).astype(jnp.int32), axis=1)
    causal = position[:, None] >= position[None, :]
    return jnp.logical_and(causal, segment[:, None] == segment[None, :])


def attend_back(query_side, key_side, value_side, grad_side, visible):
    length = query_side.shape[0]
    heads_of_query = query_side.shape[1] // HEAD_WIDTH
    scaling = 1.0 / math.sqrt(HEAD_WIDTH)

    def one_head(head_index, totals):
        query_grads, key_grads, value_gradient = totals
        query_rows = lax.dynamic_slice_in_dim(query_side, head_index * HEAD_WIDTH, HEAD_WIDTH, 1)
        grad_rows = lax.dynamic_slice_in_dim(grad_side, head_index * HEAD_WIDTH, HEAD_WIDTH, 1)
        scores = (
            jnp.einsum("id,jd->ij", query_rows, key_side, preferred_element_type=jnp.float32)
            * scaling
        )
        scores = jnp.where(visible, scores, masked_score)
        row_max = jnp.max(scores, axis=1, keepdims=True)
        weights = jnp.exp(scores - row_max)
        attn_probs = weights / jnp.sum(weights, axis=1, keepdims=True)
        probs_low = attn_probs.astype(jnp.bfloat16)
        value_part = jnp.einsum(
            "ij,id->jd", probs_low, grad_rows, preferred_element_type=jnp.float32
        )
        prob_grads = jnp.einsum(
            "id,jd->ij", grad_rows, value_side, preferred_element_type=jnp.float32
        )
        row_delta = jnp.sum(attn_probs * prob_grads, axis=1, keepdims=True)
        score_grads = (attn_probs * (prob_grads - row_delta) * scaling).astype(jnp.bfloat16)
        query_part = jnp.dot(score_grads, key_side, preferred_element_type=jnp.float32)
        key_part = jnp.einsum(
            "ij,id->jd", score_grads, query_rows, preferred_element_type=jnp.float32
        )
        query_grads = lax.dynamic_update_slice_in_dim(
            query_grads, query_part.astype(jnp.bfloat16), head_index * HEAD_WIDTH, 1
        )
        key_grads = key_grads + key_part
        value_gradient = value_gradient + value_part
        return (query_grads, key_grads, value_gradient)

    initial = (
        jnp.zeros((length, query_side.shape[1]), jnp.bfloat16),
        jnp.zeros((length, key_side.shape[1]), jnp.float32),
        jnp.zeros((length, value_side.shape[1]), jnp.float32),
    )
    return lax.fori_loop(0, heads_of_query, one_head, initial)


BLOCK_ROWS = 128


def attend_kernel(seg_row_ref, seg_col_ref, q_ref, g_ref, k_ref, v_ref, dq_ref, dk_ref, dv_ref):
    scaling = 1.0 / math.sqrt(HEAD_WIDTH)
    length = q_ref.shape[0]

    @pl.when(pl.program_id(0) == 0)
    def _():
        dk_ref[...] = jnp.zeros_like(dk_ref)
        dv_ref[...] = jnp.zeros_like(dv_ref)

    for block in range(length // BLOCK_ROWS):
        rows = pl.ds(block * BLOCK_ROWS, BLOCK_ROWS)
        span = (block + 1) * BLOCK_ROWS
        keys = k_ref[0:span, :]
        vals = v_ref[0:span, :]
        q_rows = q_ref[rows, :]
        g_rows = g_ref[rows, :]
        scores = lax.dot_general(
            q_rows, keys, (((1,), (1,)), ((), ())), preferred_element_type=jnp.float32
        ) * scaling
        row_pos = block * BLOCK_ROWS + lax.broadcasted_iota(jnp.int32, (BLOCK_ROWS, span), 0)
        col_pos = lax.broadcasted_iota(jnp.int32, (BLOCK_ROWS, span), 1)
        same = seg_row_ref[rows, :] == seg_col_ref[:, 0:span]
        visible = jnp.logical_and(row_pos >= col_pos, same)
        scores = jnp.where(visible, scores, masked_score)
        row_max = jnp.max(scores, axis=1, keepdims=True)
        weights = jnp.exp(scores - row_max)
        probs = weights * (1.0 / jnp.sum(weights, axis=1, keepdims=True))
        probs_low = probs.astype(jnp.bfloat16)
        dv_ref[0:span, :] += lax.dot_general(
            probs_low, g_rows, (((0,), (0,)), ((), ())), preferred_element_type=jnp.float32
        )
        prob_grads = lax.dot_general(
            g_rows, vals, (((1,), (1,)), ((), ())), preferred_element_type=jnp.float32
        )
        row_delta = jnp.sum(probs * prob_grads, axis=1, keepdims=True)
        score_grads = (probs * (prob_grads - row_delta) * scaling).astype(jnp.bfloat16)
        dq_ref[rows, :] = jnp.dot(
            score_grads, keys, preferred_element_type=jnp.float32
        ).astype(dq_ref.dtype)
        dk_ref[0:span, :] += lax.dot_general(
            score_grads, q_rows, (((0,), (0,)), ((), ())), preferred_element_type=jnp.float32
        )


def attend_back_kernel(gathered, segment, heads_of_query, q_block, g_block, k_block, v_block):
    length = gathered.shape[0]
    seg_row = segment.reshape(length, 1)
    seg_col = segment.reshape(1, length)
    full = lambda h: (0, 0)
    col = lambda b: pl.BlockSpec((length, HEAD_WIDTH), lambda h: (0, b))
    flops = 5 * 2 * length * length * HEAD_WIDTH * heads_of_query * 9 // 16
    return pl.pallas_call(
        attend_kernel,
        grid=(heads_of_query,),
        in_specs=[
            pl.BlockSpec((length, 1), full),
            pl.BlockSpec((1, length), full),
            pl.BlockSpec((length, HEAD_WIDTH), lambda h: (0, q_block + h)),
            pl.BlockSpec((length, HEAD_WIDTH), lambda h: (0, g_block + h)),
            col(k_block),
            col(v_block),
        ],
        out_specs=[
            pl.BlockSpec((length, HEAD_WIDTH), lambda h: (0, h)),
            pl.BlockSpec((length, HEAD_WIDTH), full),
            pl.BlockSpec((length, HEAD_WIDTH), full),
        ],
        out_shape=[
            jax.ShapeDtypeStruct((length, heads_of_query * HEAD_WIDTH), jnp.bfloat16),
            jax.ShapeDtypeStruct((length, HEAD_WIDTH), jnp.float32),
            jax.ShapeDtypeStruct((length, HEAD_WIDTH), jnp.float32),
        ],
        compiler_params=pltpu.CompilerParams(
            dimension_semantics=("arbitrary",), vmem_limit_bytes=48 * 1024 * 1024
        ),
        cost_estimate=pl.CostEstimate(
            flops=flops,
            transcendentals=length * length * heads_of_query * 9 // 16,
            bytes_accessed=length * HEAD_WIDTH * (2 * 2 * heads_of_query + 2 * 2 + 2 * heads_of_query + 8),
        ),
    )(seg_row, seg_col, gathered, gathered, gathered, gathered)


def route(payload, order):
    prompt_count = lax.axis_size("dp")
    flat = payload.reshape(prompt_count, -1)
    spread = lax.all_to_all(flat, "dp", 0, 0, tiled=True)
    routed = jnp.take(spread, order, axis=0)
    back = lax.all_to_all(routed, "dp", 0, 0, tiled=True)
    return back.reshape(payload.shape)


def pick_heads(block, heads):
    parts = [
        lax.dynamic_slice_in_dim(block, heads[k] * HEAD_WIDTH, HEAD_WIDTH, 1)
        for k in range(KNOCKOUT_COUNT)
    ]
    return jnp.stack(parts, axis=1)


def per_device(queries, keys, values, output_gradient, seg_lengths, knocked, source):
    sequence_count = lax.axis_size("seq")
    prompt_count = lax.axis_size("dp")
    tok_rows = queries.shape[0]
    length = tok_rows * sequence_count
    prompt_index = lax.axis_index("dp")
    prompt_ids = jnp.arange(prompt_count, dtype=jnp.int32)
    consumer = jnp.sum(
        jnp.where(source[None, :] == prompt_ids[:, None], prompt_ids[None, :], 0), axis=1
    )
    my_knock = knocked[prompt_index]
    their_knock = knocked[consumer[prompt_index]]
    head_ids = jnp.arange(KEY_VALUE_HEADS, dtype=jnp.int32)[None, :, None]

    outgoing = pick_heads(keys, their_knock)
    fetched = route(outgoing, source)
    keys3 = keys.reshape(tok_rows, KEY_VALUE_HEADS, HEAD_WIDTH)
    used3 = keys3
    for k in range(KNOCKOUT_COUNT - 1, -1, -1):
        used3 = jnp.where(head_ids == my_knock[k], fetched[:, k : k + 1, :], used3)
    used_keys = used3.reshape(tok_rows, -1)

    def cols(x):
        return x.reshape(tok_rows, sequence_count, -1)

    packed = jnp.concatenate(
        [cols(queries), cols(output_gradient), cols(used_keys), cols(values)], axis=2
    )
    widths = (
        queries.shape[1] // sequence_count,
        output_gradient.shape[1] // sequence_count,
        keys.shape[1] // sequence_count,
        values.shape[1] // sequence_count,
    )
    gathered = lax.all_to_all(packed, "seq", split_axis=1, concat_axis=0, tiled=True)
    gathered = gathered.reshape(length, -1)
    offsets = [0]
    for w in widths:
        offsets.append(offsets[-1] + w)

    doc_ends = jnp.cumsum(seg_lengths[0])
    position = jnp.arange(length, dtype=jnp.int32)
    segment = jnp.sum((position[:, None] >= doc_ends[None, :]).astype(jnp.int32), axis=1)
    heads_here = widths[0] // HEAD_WIDTH
    query_grads, key_grads, value_gradient = attend_back_kernel(
        gathered, segment, heads_here, 0, heads_here, 2 * heads_here, 2 * heads_here + 1
    )

    low = jnp.concatenate(
        [query_grads, value_gradient.astype(jnp.bfloat16), key_grads.astype(jnp.bfloat16)], axis=1
    )
    low_back = lax.all_to_all(low, "seq", split_axis=0, concat_axis=1, tiled=True)
    low_back = low_back.reshape(tok_rows, sequence_count, -1)
    v_end = widths[0] + widths[3]
    query_out = low_back[:, :, : widths[0]].reshape(tok_rows, -1)
    value_out = low_back[:, :, widths[0] : v_end].reshape(tok_rows, -1)
    key_back = low_back[:, :, v_end:].reshape(tok_rows, -1)

    returning = pick_heads(key_back, my_knock)
    returned = route(returning, consumer)
    key3 = key_back.reshape(tok_rows, KEY_VALUE_HEADS, HEAD_WIDTH)
    own = key3
    for k in range(KNOCKOUT_COUNT):
        own = jnp.where(head_ids == my_knock[k], jnp.zeros_like(own), own)
    extra = jnp.zeros_like(key3)
    for k in range(KNOCKOUT_COUNT):
        extra = jnp.where(head_ids == their_knock[k], returned[:, k : k + 1, :], extra)
    key_out = (own.astype(jnp.float32) + extra.astype(jnp.float32)).astype(jnp.bfloat16).reshape(tok_rows, -1)
    return (query_out, key_out, value_out)


def solution(mesh):
    placed = (
        P(("dp", "seq"), None),
        P(("dp", "seq"), None),
        P(("dp", "seq"), None),
        P(("dp", "seq"), None),
        P("dp", None),
        P(),
        P(),
    )
    return jax.shard_map(
        per_device,
        mesh=mesh,
        in_specs=placed,
        out_specs=(P(("dp", "seq"), None), P(("dp", "seq"), None), P(("dp", "seq"), None)),
        check_vma=False,
    )
```

```python
import math

import jax
import jax.numpy as jnp
from jax import lax
from jax.experimental import pallas as pl
from jax.experimental.pallas import tpu as pltpu
from jax.sharding import PartitionSpec as P

KEY_VALUE_HEADS = 8
HEAD_WIDTH = 128
KNOCKOUT_COUNT = 2


masked_score = -1e30


def document_mask(lengths, length):
    doc_ends = jnp.cumsum(lengths)
    position = jnp.arange(length, dtype=jnp.int32)
    segment = jnp.sum((position[:, None] >= doc_ends[None, :]).astype(jnp.int32), axis=1)
    causal = position[:, None] >= position[None, :]
    return jnp.logical_and(causal, segment[:, None] == segment[None, :])


def attend_back(query_side, key_side, value_side, grad_side, visible):
    length = query_side.shape[0]
    heads_of_query = query_side.shape[1] // HEAD_WIDTH
    scaling = 1.0 / math.sqrt(HEAD_WIDTH)

    def one_head(head_index, totals):
        query_grads, key_grads, value_gradient = totals
        query_rows = lax.dynamic_slice_in_dim(query_side, head_index * HEAD_WIDTH, HEAD_WIDTH, 1)
        grad_rows = lax.dynamic_slice_in_dim(grad_side, head_index * HEAD_WIDTH, HEAD_WIDTH, 1)
        scores = (
            jnp.einsum("id,jd->ij", query_rows, key_side, preferred_element_type=jnp.float32)
            * scaling
        )
        scores = jnp.where(visible, scores, masked_score)
        row_max = jnp.max(scores, axis=1, keepdims=True)
        weights = jnp.exp(scores - row_max)
        attn_probs = weights / jnp.sum(weights, axis=1, keepdims=True)
        probs_low = attn_probs.astype(jnp.bfloat16)
        value_part = jnp.einsum(
            "ij,id->jd", probs_low, grad_rows, preferred_element_type=jnp.float32
        )
        prob_grads = jnp.einsum(
            "id,jd->ij", grad_rows, value_side, preferred_element_type=jnp.float32
        )
        row_delta = jnp.sum(attn_probs * prob_grads, axis=1, keepdims=True)
        score_grads = (attn_probs * (prob_grads - row_delta) * scaling).astype(jnp.bfloat16)
        query_part = jnp.dot(score_grads, key_side, preferred_element_type=jnp.float32)
        key_part = jnp.einsum(
            "ij,id->jd", score_grads, query_rows, preferred_element_type=jnp.float32
        )
        query_grads = lax.dynamic_update_slice_in_dim(
            query_grads, query_part.astype(jnp.bfloat16), head_index * HEAD_WIDTH, 1
        )
        key_grads = key_grads + key_part
        value_gradient = value_gradient + value_part
        return (query_grads, key_grads, value_gradient)

    initial = (
        jnp.zeros((length, query_side.shape[1]), jnp.bfloat16),
        jnp.zeros((length, key_side.shape[1]), jnp.float32),
        jnp.zeros((length, value_side.shape[1]), jnp.float32),
    )
    return lax.fori_loop(0, heads_of_query, one_head, initial)


BLOCK_ROWS = 256


def attend_kernel(seg_row_ref, seg_col_ref, q_ref, g_ref, k_ref, v_ref, dq_ref, dk_ref, dv_ref):
    scaling = 1.0 / math.sqrt(HEAD_WIDTH)
    length = q_ref.shape[0]

    @pl.when(pl.program_id(0) == 0)
    def _():
        dk_ref[...] = jnp.zeros_like(dk_ref)
        dv_ref[...] = jnp.zeros_like(dv_ref)

    for block in range(length // BLOCK_ROWS):
        rows = pl.ds(block * BLOCK_ROWS, BLOCK_ROWS)
        span = (block + 1) * BLOCK_ROWS
        keys = k_ref[0:span, :]
        vals = v_ref[0:span, :]
        q_rows = q_ref[rows, :]
        g_rows = g_ref[rows, :]
        scores = lax.dot_general(
            keys, q_rows, (((1,), (1,)), ((), ())), preferred_element_type=jnp.float32
        ) * scaling
        key_pos = lax.broadcasted_iota(jnp.int32, (span, BLOCK_ROWS), 0)
        query_pos = block * BLOCK_ROWS + lax.broadcasted_iota(jnp.int32, (span, BLOCK_ROWS), 1)
        same = seg_row_ref[0:span, :] == seg_col_ref[:, rows]
        visible = jnp.logical_and(query_pos >= key_pos, same)
        scores = jnp.where(visible, scores, masked_score)
        col_max = jnp.max(scores, axis=0, keepdims=True)
        weights = jnp.exp(scores - col_max)
        probs = weights / jnp.sum(weights, axis=0, keepdims=True)
        probs_low = probs.astype(jnp.bfloat16)
        dv_ref[0:span, :] += jnp.dot(probs_low, g_rows, preferred_element_type=jnp.float32)
        prob_grads = lax.dot_general(
            vals, g_rows, (((1,), (1,)), ((), ())), preferred_element_type=jnp.float32
        )
        col_delta = jnp.sum(probs * prob_grads, axis=0, keepdims=True)
        score_grads = (probs * (prob_grads - col_delta) * scaling).astype(jnp.bfloat16)
        dq_ref[rows, :] = lax.dot_general(
            score_grads, keys, (((0,), (0,)), ((), ())), preferred_element_type=jnp.float32
        ).astype(dq_ref.dtype)
        dk_ref[0:span, :] += jnp.dot(score_grads, q_rows, preferred_element_type=jnp.float32)


def attend_back_kernel(gathered, segment, heads_of_query, q_block, g_block, k_block, v_block):
    length = gathered.shape[0]
    seg_row = segment.reshape(length, 1)
    seg_col = segment.reshape(1, length)
    full = lambda h: (0, 0)
    col = lambda b: pl.BlockSpec((length, HEAD_WIDTH), lambda h: (0, b))
    flops = 5 * 2 * length * length * HEAD_WIDTH * heads_of_query * 10 // 16
    return pl.pallas_call(
        attend_kernel,
        grid=(heads_of_query,),
        in_specs=[
            pl.BlockSpec((length, 1), full),
            pl.BlockSpec((1, length), full),
            pl.BlockSpec((length, HEAD_WIDTH), lambda h: (0, q_block + h)),
            pl.BlockSpec((length, HEAD_WIDTH), lambda h: (0, g_block + h)),
            col(k_block),
            col(v_block),
        ],
        out_specs=[
            pl.BlockSpec((length, HEAD_WIDTH), lambda h: (0, h)),
            pl.BlockSpec((length, HEAD_WIDTH), full),
            pl.BlockSpec((length, HEAD_WIDTH), full),
        ],
        out_shape=[
            jax.ShapeDtypeStruct((length, heads_of_query * HEAD_WIDTH), jnp.bfloat16),
            jax.ShapeDtypeStruct((length, HEAD_WIDTH), jnp.float32),
            jax.ShapeDtypeStruct((length, HEAD_WIDTH), jnp.float32),
        ],
        compiler_params=pltpu.CompilerParams(
            dimension_semantics=("arbitrary",), vmem_limit_bytes=48 * 1024 * 1024
        ),
        cost_estimate=pl.CostEstimate(
            flops=flops,
            transcendentals=length * length * heads_of_query * 10 // 16,
            bytes_accessed=length * HEAD_WIDTH * (2 * 2 * heads_of_query + 2 * 2 + 2 * heads_of_query + 8),
        ),
    )(seg_row, seg_col, gathered, gathered, gathered, gathered)


def route(payload, order):
    prompt_count = lax.axis_size("dp")
    flat = payload.reshape(prompt_count, -1)
    spread = lax.all_to_all(flat, "dp", 0, 0, tiled=True)
    routed = jnp.take(spread, order, axis=0)
    back = lax.all_to_all(routed, "dp", 0, 0, tiled=True)
    return back.reshape(payload.shape)


def pick_heads(block, heads):
    parts = [
        lax.dynamic_slice_in_dim(block, heads[k] * HEAD_WIDTH, HEAD_WIDTH, 1)
        for k in range(KNOCKOUT_COUNT)
    ]
    return jnp.stack(parts, axis=1)


def per_device(queries, keys, values, output_gradient, seg_lengths, knocked, source):
    sequence_count = lax.axis_size("seq")
    prompt_count = lax.axis_size("dp")
    tok_rows = queries.shape[0]
    length = tok_rows * sequence_count
    prompt_index = lax.axis_index("dp")
    prompt_ids = jnp.arange(prompt_count, dtype=jnp.int32)
    consumer = jnp.sum(
        jnp.where(source[None, :] == prompt_ids[:, None], prompt_ids[None, :], 0), axis=1
    )
    my_knock = knocked[prompt_index]
    their_knock = knocked[consumer[prompt_index]]
    head_ids = jnp.arange(KEY_VALUE_HEADS, dtype=jnp.int32)[None, :, None]

    outgoing = pick_heads(keys, their_knock)
    fetched = route(outgoing, source)
    keys3 = keys.reshape(tok_rows, KEY_VALUE_HEADS, HEAD_WIDTH)
    used3 = keys3
    for k in range(KNOCKOUT_COUNT - 1, -1, -1):
        used3 = jnp.where(head_ids == my_knock[k], fetched[:, k : k + 1, :], used3)
    used_keys = used3.reshape(tok_rows, -1)

    def cols(x):
        return x.reshape(tok_rows, sequence_count, -1)

    packed = jnp.concatenate(
        [cols(queries), cols(output_gradient), cols(used_keys), cols(values)], axis=2
    )
    widths = (
        queries.shape[1] // sequence_count,
        output_gradient.shape[1] // sequence_count,
        keys.shape[1] // sequence_count,
        values.shape[1] // sequence_count,
    )
    gathered = lax.all_to_all(packed, "seq", split_axis=1, concat_axis=0, tiled=True)
    gathered = gathered.reshape(length, -1)
    offsets = [0]
    for w in widths:
        offsets.append(offsets[-1] + w)

    doc_ends = jnp.cumsum(seg_lengths[0])
    position = jnp.arange(length, dtype=jnp.int32)
    segment = jnp.sum((position[:, None] >= doc_ends[None, :]).astype(jnp.int32), axis=1)
    heads_here = widths[0] // HEAD_WIDTH
    query_grads, key_grads, value_gradient = attend_back_kernel(
        gathered, segment, heads_here, 0, heads_here, 2 * heads_here, 2 * heads_here + 1
    )

    low = jnp.concatenate(
        [query_grads, value_gradient.astype(jnp.bfloat16), key_grads.astype(jnp.bfloat16)], axis=1
    )
    low_back = lax.all_to_all(low, "seq", split_axis=0, concat_axis=1, tiled=True)
    low_back = low_back.reshape(tok_rows, sequence_count, -1)
    v_end = widths[0] + widths[3]
    query_out = low_back[:, :, : widths[0]].reshape(tok_rows, -1)
    value_out = low_back[:, :, widths[0] : v_end].reshape(tok_rows, -1)
    key_back = low_back[:, :, v_end:].reshape(tok_rows, -1)

    returning = pick_heads(key_back, my_knock)
    returned = route(returning, consumer)
    key3 = key_back.reshape(tok_rows, KEY_VALUE_HEADS, HEAD_WIDTH)
    own = key3
    for k in range(KNOCKOUT_COUNT):
        own = jnp.where(head_ids == my_knock[k], jnp.zeros_like(own), own)
    extra = jnp.zeros_like(key3)
    for k in range(KNOCKOUT_COUNT):
        extra = jnp.where(head_ids == their_knock[k], returned[:, k : k + 1, :], extra)
    key_out = (own.astype(jnp.float32) + extra.astype(jnp.float32)).astype(jnp.bfloat16).reshape(tok_rows, -1)
    return (query_out, key_out, value_out)


def solution(mesh):
    placed = (
        P(("dp", "seq"), None),
        P(("dp", "seq"), None),
        P(("dp", "seq"), None),
        P(("dp", "seq"), None),
        P("dp", None),
        P(),
        P(),
    )
    return jax.shard_map(
        per_device,
        mesh=mesh,
        in_specs=placed,
        out_specs=(P(("dp", "seq"), None), P(("dp", "seq"), None), P(("dp", "seq"), None)),
        check_vma=False,
    )
```

```python
import math

import jax
import jax.numpy as jnp
from jax import lax
from jax.experimental import pallas as pl
from jax.experimental.pallas import tpu as pltpu
from jax.sharding import PartitionSpec as P

KEY_VALUE_HEADS = 8
HEAD_WIDTH = 128
KNOCKOUT_COUNT = 2


masked_score = -1e30


def document_mask(lengths, length):
    doc_ends = jnp.cumsum(lengths)
    position = jnp.arange(length, dtype=jnp.int32)
    segment = jnp.sum((position[:, None] >= doc_ends[None, :]).astype(jnp.int32), axis=1)
    causal = position[:, None] >= position[None, :]
    return jnp.logical_and(causal, segment[:, None] == segment[None, :])


def attend_back(query_side, key_side, value_side, grad_side, visible):
    length = query_side.shape[0]
    heads_of_query = query_side.shape[1] // HEAD_WIDTH
    scaling = 1.0 / math.sqrt(HEAD_WIDTH)

    def one_head(head_index, totals):
        query_grads, key_grads, value_gradient = totals
        query_rows = lax.dynamic_slice_in_dim(query_side, head_index * HEAD_WIDTH, HEAD_WIDTH, 1)
        grad_rows = lax.dynamic_slice_in_dim(grad_side, head_index * HEAD_WIDTH, HEAD_WIDTH, 1)
        scores = (
            jnp.einsum("id,jd->ij", query_rows, key_side, preferred_element_type=jnp.float32)
            * scaling
        )
        scores = jnp.where(visible, scores, masked_score)
        row_max = jnp.max(scores, axis=1, keepdims=True)
        weights = jnp.exp(scores - row_max)
        attn_probs = weights / jnp.sum(weights, axis=1, keepdims=True)
        probs_low = attn_probs.astype(jnp.bfloat16)
        value_part = jnp.einsum(
            "ij,id->jd", probs_low, grad_rows, preferred_element_type=jnp.float32
        )
        prob_grads = jnp.einsum(
            "id,jd->ij", grad_rows, value_side, preferred_element_type=jnp.float32
        )
        row_delta = jnp.sum(attn_probs * prob_grads, axis=1, keepdims=True)
        score_grads = (attn_probs * (prob_grads - row_delta) * scaling).astype(jnp.bfloat16)
        query_part = jnp.dot(score_grads, key_side, preferred_element_type=jnp.float32)
        key_part = jnp.einsum(
            "ij,id->jd", score_grads, query_rows, preferred_element_type=jnp.float32
        )
        query_grads = lax.dynamic_update_slice_in_dim(
            query_grads, query_part.astype(jnp.bfloat16), head_index * HEAD_WIDTH, 1
        )
        key_grads = key_grads + key_part
        value_gradient = value_gradient + value_part
        return (query_grads, key_grads, value_gradient)

    initial = (
        jnp.zeros((length, query_side.shape[1]), jnp.bfloat16),
        jnp.zeros((length, key_side.shape[1]), jnp.float32),
        jnp.zeros((length, value_side.shape[1]), jnp.float32),
    )
    return lax.fori_loop(0, heads_of_query, one_head, initial)


BLOCK_ROWS = 256


def attend_kernel(seg_row_ref, seg_col_ref, q_ref, g_ref, k_ref, v_ref, dq_ref, dk_ref, dv_ref):
    scaling = 1.0 / math.sqrt(HEAD_WIDTH)
    length = q_ref.shape[0]

    @pl.when(pl.program_id(0) == 0)
    def _():
        dk_ref[...] = jnp.zeros_like(dk_ref)
        dv_ref[...] = jnp.zeros_like(dv_ref)

    for block in range(length // BLOCK_ROWS):
        rows = pl.ds(block * BLOCK_ROWS, BLOCK_ROWS)
        span = (block + 1) * BLOCK_ROWS
        keys = k_ref[0:span, :]
        vals = v_ref[0:span, :]
        q_rows = q_ref[rows, :]
        g_rows = g_ref[rows, :]
        scores = lax.dot_general(
            q_rows, keys, (((1,), (1,)), ((), ())), preferred_element_type=jnp.float32
        ) * scaling
        row_pos = block * BLOCK_ROWS + lax.broadcasted_iota(jnp.int32, (BLOCK_ROWS, span), 0)
        col_pos = lax.broadcasted_iota(jnp.int32, (BLOCK_ROWS, span), 1)
        same = seg_row_ref[rows, :] == seg_col_ref[:, 0:span]
        visible = jnp.logical_and(row_pos >= col_pos, same)
        scores = jnp.where(visible, scores, masked_score)
        row_max = jnp.max(scores, axis=1, keepdims=True)
        weights = jnp.exp(scores - row_max)
        probs = weights / jnp.sum(weights, axis=1, keepdims=True)
        probs_low = probs.astype(jnp.bfloat16)
        dv_ref[0:span, :] += lax.dot_general(
            probs_low, g_rows, (((0,), (0,)), ((), ())), preferred_element_type=jnp.float32
        )
        prob_grads = lax.dot_general(
            g_rows, vals, (((1,), (1,)), ((), ())), preferred_element_type=jnp.float32
        )
        row_delta = jnp.sum(probs * prob_grads, axis=1, keepdims=True)
        score_grads = (probs * (prob_grads - row_delta) * scaling).astype(jnp.bfloat16)
        dq_ref[rows, :] = jnp.dot(
            score_grads, keys, preferred_element_type=jnp.float32
        ).astype(dq_ref.dtype)
        dk_ref[0:span, :] += lax.dot_general(
            score_grads, q_rows, (((0,), (0,)), ((), ())), preferred_element_type=jnp.float32
        )


def attend_back_kernel(gathered, segment, heads_of_query, q_block, g_block, k_block, v_block):
    length = gathered.shape[0]
    seg_row = segment.reshape(length, 1)
    seg_col = segment.reshape(1, length)
    full = lambda h: (0, 0)
    col = lambda b: pl.BlockSpec((length, HEAD_WIDTH), lambda h: (0, b))
    flops = 5 * 2 * length * length * HEAD_WIDTH * heads_of_query * 10 // 16
    return pl.pallas_call(
        attend_kernel,
        grid=(heads_of_query,),
        in_specs=[
            pl.BlockSpec((length, 1), full),
            pl.BlockSpec((1, length), full),
            pl.BlockSpec((length, HEAD_WIDTH), lambda h: (0, q_block + h)),
            pl.BlockSpec((length, HEAD_WIDTH), lambda h: (0, g_block + h)),
            col(k_block),
            col(v_block),
        ],
        out_specs=[
            pl.BlockSpec((length, HEAD_WIDTH), lambda h: (0, h)),
            pl.BlockSpec((length, HEAD_WIDTH), full),
            pl.BlockSpec((length, HEAD_WIDTH), full),
        ],
        out_shape=[
            jax.ShapeDtypeStruct((length, heads_of_query * HEAD_WIDTH), jnp.bfloat16),
            jax.ShapeDtypeStruct((length, HEAD_WIDTH), jnp.float32),
            jax.ShapeDtypeStruct((length, HEAD_WIDTH), jnp.float32),
        ],
        compiler_params=pltpu.CompilerParams(
            dimension_semantics=("arbitrary",), vmem_limit_bytes=48 * 1024 * 1024
        ),
        cost_estimate=pl.CostEstimate(
            flops=flops,
            transcendentals=length * length * heads_of_query * 10 // 16,
            bytes_accessed=length * HEAD_WIDTH * (2 * 2 * heads_of_query + 2 * 2 + 2 * heads_of_query + 8),
        ),
    )(seg_row, seg_col, gathered, gathered, gathered, gathered)


def route_block(block, order, heads):
    prompt_count = lax.axis_size("dp")
    rows = block.shape[0]
    flat = block.reshape(prompt_count, rows // prompt_count, KEY_VALUE_HEADS, HEAD_WIDTH)
    spread = lax.all_to_all(flat, "dp", 0, 0, tiled=True)
    routed = jnp.take(spread, order, axis=0)
    routed = jnp.take_along_axis(routed, heads[:, None, :, None], axis=2)
    back = lax.all_to_all(routed, "dp", 0, 0, tiled=True)
    return back.reshape(rows, KNOCKOUT_COUNT, HEAD_WIDTH)


def route(payload, order):
    prompt_count = lax.axis_size("dp")
    flat = payload.reshape(prompt_count, -1)
    spread = lax.all_to_all(flat, "dp", 0, 0, tiled=True)
    routed = jnp.take(spread, order, axis=0)
    back = lax.all_to_all(routed, "dp", 0, 0, tiled=True)
    return back.reshape(payload.shape)


def pick_heads(block, heads):
    parts = [
        lax.dynamic_slice_in_dim(block, heads[k] * HEAD_WIDTH, HEAD_WIDTH, 1)
        for k in range(KNOCKOUT_COUNT)
    ]
    return jnp.stack(parts, axis=1)


def per_device(queries, keys, values, output_gradient, seg_lengths, knocked, source):
    sequence_count = lax.axis_size("seq")
    prompt_count = lax.axis_size("dp")
    tok_rows = queries.shape[0]
    length = tok_rows * sequence_count
    prompt_index = lax.axis_index("dp")
    prompt_ids = jnp.arange(prompt_count, dtype=jnp.int32)
    consumer = jnp.zeros((prompt_count,), jnp.int32).at[source].set(prompt_ids)
    my_knock = knocked[prompt_index]
    their_knock = knocked[consumer[prompt_index]]
    head_ids = jnp.arange(KEY_VALUE_HEADS, dtype=jnp.int32)[None, :, None]

    fetched = route_block(keys, source, knocked)
    keys3 = keys.reshape(tok_rows, KEY_VALUE_HEADS, HEAD_WIDTH)
    used3 = keys3
    for k in range(KNOCKOUT_COUNT - 1, -1, -1):
        used3 = jnp.where(head_ids == my_knock[k], fetched[:, k : k + 1, :], used3)
    used_keys = used3.reshape(tok_rows, -1)

    def cols(x):
        return x.reshape(tok_rows, sequence_count, -1)

    packed = jnp.concatenate(
        [cols(queries), cols(output_gradient), cols(used_keys), cols(values)], axis=2
    )
    widths = (
        queries.shape[1] // sequence_count,
        output_gradient.shape[1] // sequence_count,
        keys.shape[1] // sequence_count,
        values.shape[1] // sequence_count,
    )
    gathered = lax.all_to_all(packed, "seq", split_axis=1, concat_axis=0, tiled=True)
    gathered = gathered.reshape(length, -1)
    offsets = [0]
    for w in widths:
        offsets.append(offsets[-1] + w)

    doc_ends = jnp.cumsum(seg_lengths[0])
    position = jnp.arange(length, dtype=jnp.int32)
    segment = jnp.sum((position[:, None] >= doc_ends[None, :]).astype(jnp.int32), axis=1)
    heads_here = widths[0] // HEAD_WIDTH
    query_grads, key_grads, value_gradient = attend_back_kernel(
        gathered, segment, heads_here, 0, heads_here, 2 * heads_here, 2 * heads_here + 1
    )

    low = jnp.concatenate(
        [query_grads, value_gradient.astype(jnp.bfloat16), key_grads.astype(jnp.bfloat16)], axis=1
    )
    low_back = lax.all_to_all(low, "seq", split_axis=0, concat_axis=1, tiled=True)
    low_back = low_back.reshape(tok_rows, sequence_count, -1)
    v_end = widths[0] + widths[3]
    query_out = low_back[:, :, : widths[0]].reshape(tok_rows, -1)
    value_out = low_back[:, :, widths[0] : v_end].reshape(tok_rows, -1)
    key_back = low_back[:, :, v_end:].reshape(tok_rows, -1)

    returning = pick_heads(key_back, my_knock)
    returned = route(returning, consumer)
    key3 = key_back.reshape(tok_rows, KEY_VALUE_HEADS, HEAD_WIDTH)
    own = key3
    for k in range(KNOCKOUT_COUNT):
        own = jnp.where(head_ids == my_knock[k], jnp.zeros_like(own), own)
    extra = jnp.zeros_like(key3)
    for k in range(KNOCKOUT_COUNT):
        extra = jnp.where(head_ids == their_knock[k], returned[:, k : k + 1, :], extra)
    key_out = (own.astype(jnp.float32) + extra.astype(jnp.float32)).astype(jnp.bfloat16).reshape(tok_rows, -1)
    return (query_out, key_out, value_out)


def solution(mesh):
    placed = (
        P(("dp", "seq"), None),
        P(("dp", "seq"), None),
        P(("dp", "seq"), None),
        P(("dp", "seq"), None),
        P("dp", None),
        P(),
        P(),
    )
    return jax.shard_map(
        per_device,
        mesh=mesh,
        in_specs=placed,
        out_specs=(P(("dp", "seq"), None), P(("dp", "seq"), None), P(("dp", "seq"), None)),
        check_vma=False,
    )
```

```python
import math

import jax
import jax.numpy as jnp
from jax import lax
from jax.experimental import pallas as pl
from jax.experimental.pallas import tpu as pltpu
from jax.sharding import PartitionSpec as P

KEY_VALUE_HEADS = 8
HEAD_WIDTH = 128
KNOCKOUT_COUNT = 2


masked_score = -1e30


def document_mask(lengths, length):
    doc_ends = jnp.cumsum(lengths)
    position = jnp.arange(length, dtype=jnp.int32)
    segment = jnp.sum((position[:, None] >= doc_ends[None, :]).astype(jnp.int32), axis=1)
    causal = position[:, None] >= position[None, :]
    return jnp.logical_and(causal, segment[:, None] == segment[None, :])


def attend_back(query_side, key_side, value_side, grad_side, visible):
    length = query_side.shape[0]
    heads_of_query = query_side.shape[1] // HEAD_WIDTH
    scaling = 1.0 / math.sqrt(HEAD_WIDTH)

    def one_head(head_index, totals):
        query_grads, key_grads, value_gradient = totals
        query_rows = lax.dynamic_slice_in_dim(query_side, head_index * HEAD_WIDTH, HEAD_WIDTH, 1)
        grad_rows = lax.dynamic_slice_in_dim(grad_side, head_index * HEAD_WIDTH, HEAD_WIDTH, 1)
        scores = (
            jnp.einsum("id,jd->ij", query_rows, key_side, preferred_element_type=jnp.float32)
            * scaling
        )
        scores = jnp.where(visible, scores, masked_score)
        row_max = jnp.max(scores, axis=1, keepdims=True)
        weights = jnp.exp(scores - row_max)
        attn_probs = weights / jnp.sum(weights, axis=1, keepdims=True)
        probs_low = attn_probs.astype(jnp.bfloat16)
        value_part = jnp.einsum(
            "ij,id->jd", probs_low, grad_rows, preferred_element_type=jnp.float32
        )
        prob_grads = jnp.einsum(
            "id,jd->ij", grad_rows, value_side, preferred_element_type=jnp.float32
        )
        row_delta = jnp.sum(attn_probs * prob_grads, axis=1, keepdims=True)
        score_grads = (attn_probs * (prob_grads - row_delta) * scaling).astype(jnp.bfloat16)
        query_part = jnp.dot(score_grads, key_side, preferred_element_type=jnp.float32)
        key_part = jnp.einsum(
            "ij,id->jd", score_grads, query_rows, preferred_element_type=jnp.float32
        )
        query_grads = lax.dynamic_update_slice_in_dim(
            query_grads, query_part.astype(jnp.bfloat16), head_index * HEAD_WIDTH, 1
        )
        key_grads = key_grads + key_part
        value_gradient = value_gradient + value_part
        return (query_grads, key_grads, value_gradient)

    initial = (
        jnp.zeros((length, query_side.shape[1]), jnp.bfloat16),
        jnp.zeros((length, key_side.shape[1]), jnp.float32),
        jnp.zeros((length, value_side.shape[1]), jnp.float32),
    )
    return lax.fori_loop(0, heads_of_query, one_head, initial)


BLOCK_ROWS = 256


def attend_kernel(seg_row_ref, seg_col_ref, q_ref, g_ref, k_ref, v_ref, out_ref, dk_acc, dv_acc):
    scaling = 1.0 / math.sqrt(HEAD_WIDTH)
    length = q_ref.shape[0]
    head = pl.program_id(0)
    heads = pl.num_programs(0)

    @pl.when(head == 0)
    def _():
        dk_acc[...] = jnp.zeros_like(dk_acc)
        dv_acc[...] = jnp.zeros_like(dv_acc)

    dq_cols = pl.ds(pl.multiple_of(head * HEAD_WIDTH, HEAD_WIDTH), HEAD_WIDTH)
    for block in range(length // BLOCK_ROWS):
        rows = pl.ds(block * BLOCK_ROWS, BLOCK_ROWS)
        span = (block + 1) * BLOCK_ROWS
        keys = k_ref[0:span, :]
        vals = v_ref[0:span, :]
        q_rows = q_ref[rows, :]
        g_rows = g_ref[rows, :]
        scores = lax.dot_general(
            q_rows, keys, (((1,), (1,)), ((), ())), preferred_element_type=jnp.float32
        ) * scaling
        row_pos = block * BLOCK_ROWS + lax.broadcasted_iota(jnp.int32, (BLOCK_ROWS, span), 0)
        col_pos = lax.broadcasted_iota(jnp.int32, (BLOCK_ROWS, span), 1)
        same = seg_row_ref[rows, :] == seg_col_ref[:, 0:span]
        visible = jnp.logical_and(row_pos >= col_pos, same)
        scores = jnp.where(visible, scores, masked_score)
        row_max = jnp.max(scores, axis=1, keepdims=True)
        weights = jnp.exp(scores - row_max)
        probs = weights / jnp.sum(weights, axis=1, keepdims=True)
        probs_low = probs.astype(jnp.bfloat16)
        dv_acc[0:span, :] += lax.dot_general(
            probs_low, g_rows, (((0,), (0,)), ((), ())), preferred_element_type=jnp.float32
        )
        prob_grads = lax.dot_general(
            g_rows, vals, (((1,), (1,)), ((), ())), preferred_element_type=jnp.float32
        )
        row_delta = jnp.sum(probs * prob_grads, axis=1, keepdims=True)
        score_grads = (probs * (prob_grads - row_delta) * scaling).astype(jnp.bfloat16)
        out_ref[rows, dq_cols] = jnp.dot(
            score_grads, keys, preferred_element_type=jnp.float32
        ).astype(out_ref.dtype)
        dk_acc[0:span, :] += lax.dot_general(
            score_grads, q_rows, (((0,), (0,)), ((), ())), preferred_element_type=jnp.float32
        )

    @pl.when(head == heads - 1)
    def _():
        base = out_ref.shape[1] - 2 * HEAD_WIDTH
        out_ref[:, base : base + HEAD_WIDTH] = dv_acc[...].astype(out_ref.dtype)
        out_ref[:, base + HEAD_WIDTH :] = dk_acc[...].astype(out_ref.dtype)


def attend_back_kernel(gathered, segment, heads_of_query, q_block, g_block, k_block, v_block):
    length = gathered.shape[0]
    seg_row = segment.reshape(length, 1)
    seg_col = segment.reshape(1, length)
    full = lambda h: (0, 0)
    col = lambda b: pl.BlockSpec((length, HEAD_WIDTH), lambda h: (0, b))
    width = (heads_of_query + 2) * HEAD_WIDTH
    flops = 5 * 2 * length * length * HEAD_WIDTH * heads_of_query * 10 // 16
    return pl.pallas_call(
        attend_kernel,
        grid=(heads_of_query,),
        in_specs=[
            pl.BlockSpec((length, 1), full),
            pl.BlockSpec((1, length), full),
            pl.BlockSpec((length, HEAD_WIDTH), lambda h: (0, q_block + h)),
            pl.BlockSpec((length, HEAD_WIDTH), lambda h: (0, g_block + h)),
            col(k_block),
            col(v_block),
        ],
        out_specs=pl.BlockSpec((length, width), full),
        out_shape=jax.ShapeDtypeStruct((length, width), jnp.bfloat16),
        scratch_shapes=[
            pltpu.VMEM((length, HEAD_WIDTH), jnp.float32),
            pltpu.VMEM((length, HEAD_WIDTH), jnp.float32),
        ],
        compiler_params=pltpu.CompilerParams(
            dimension_semantics=("arbitrary",), vmem_limit_bytes=48 * 1024 * 1024
        ),
        cost_estimate=pl.CostEstimate(
            flops=flops,
            transcendentals=length * length * heads_of_query * 10 // 16,
            bytes_accessed=length * HEAD_WIDTH * (2 * 2 * heads_of_query + 2 * 2 + 2 * width // HEAD_WIDTH),
        ),
    )(seg_row, seg_col, gathered, gathered, gathered, gathered)

def route_block(block, order, heads):
    prompt_count = lax.axis_size("dp")
    rows = block.shape[0]
    flat = block.reshape(prompt_count, rows // prompt_count, KEY_VALUE_HEADS, HEAD_WIDTH)
    spread = lax.all_to_all(flat, "dp", 0, 0, tiled=True)
    routed = jnp.take(spread, order, axis=0)
    routed = jnp.take_along_axis(routed, heads[:, None, :, None], axis=2)
    back = lax.all_to_all(routed, "dp", 0, 0, tiled=True)
    return back.reshape(rows, KNOCKOUT_COUNT, HEAD_WIDTH)


def route(payload, order):
    prompt_count = lax.axis_size("dp")
    flat = payload.reshape(prompt_count, -1)
    spread = lax.all_to_all(flat, "dp", 0, 0, tiled=True)
    routed = jnp.take(spread, order, axis=0)
    back = lax.all_to_all(routed, "dp", 0, 0, tiled=True)
    return back.reshape(payload.shape)


def pick_heads(block, heads):
    parts = [
        lax.dynamic_slice_in_dim(block, heads[k] * HEAD_WIDTH, HEAD_WIDTH, 1)
        for k in range(KNOCKOUT_COUNT)
    ]
    return jnp.stack(parts, axis=1)


def per_device(queries, keys, values, output_gradient, seg_lengths, knocked, source):
    sequence_count = lax.axis_size("seq")
    prompt_count = lax.axis_size("dp")
    tok_rows = queries.shape[0]
    length = tok_rows * sequence_count
    prompt_index = lax.axis_index("dp")
    prompt_ids = jnp.arange(prompt_count, dtype=jnp.int32)
    consumer = jnp.zeros((prompt_count,), jnp.int32).at[source].set(prompt_ids)
    my_knock = knocked[prompt_index]
    their_knock = knocked[consumer[prompt_index]]
    head_ids = jnp.arange(KEY_VALUE_HEADS, dtype=jnp.int32)[None, :, None]

    fetched = route_block(keys, source, knocked)
    keys3 = keys.reshape(tok_rows, KEY_VALUE_HEADS, HEAD_WIDTH)
    used3 = keys3
    for k in range(KNOCKOUT_COUNT - 1, -1, -1):
        used3 = jnp.where(head_ids == my_knock[k], fetched[:, k : k + 1, :], used3)
    used_keys = used3.reshape(tok_rows, -1)

    def cols(x):
        return x.reshape(tok_rows, sequence_count, -1)

    pre = jnp.concatenate(
        [cols(queries), cols(output_gradient), jnp.zeros_like(cols(keys)), cols(values)], axis=2
    )
    pre = lax.optimization_barrier(pre)
    key_at = (queries.shape[1] + output_gradient.shape[1]) // sequence_count
    packed = lax.dynamic_update_slice(pre, cols(used_keys), (0, 0, key_at))
    widths = (
        queries.shape[1] // sequence_count,
        output_gradient.shape[1] // sequence_count,
        keys.shape[1] // sequence_count,
        values.shape[1] // sequence_count,
    )
    gathered = lax.all_to_all(packed, "seq", split_axis=1, concat_axis=0, tiled=True)
    gathered = gathered.reshape(length, -1)
    offsets = [0]
    for w in widths:
        offsets.append(offsets[-1] + w)

    doc_ends = jnp.cumsum(seg_lengths[0])
    position = jnp.arange(length, dtype=jnp.int32)
    segment = jnp.sum((position[:, None] >= doc_ends[None, :]).astype(jnp.int32), axis=1)
    heads_here = widths[0] // HEAD_WIDTH
    low = attend_back_kernel(
        gathered, segment, heads_here, 0, heads_here, 2 * heads_here, 2 * heads_here + 1
    )

    low_back = lax.all_to_all(low, "seq", split_axis=0, concat_axis=1, tiled=True)
    low_back = low_back.reshape(tok_rows, sequence_count, -1)
    v_end = widths[0] + widths[3]
    query_out = low_back[:, :, : widths[0]].reshape(tok_rows, -1)
    value_out = low_back[:, :, widths[0] : v_end].reshape(tok_rows, -1)
    key_back = low_back[:, :, v_end:].reshape(tok_rows, -1)

    returning = pick_heads(key_back, my_knock)
    returned = route(returning, consumer)
    key3 = key_back.reshape(tok_rows, KEY_VALUE_HEADS, HEAD_WIDTH)
    own = key3
    for k in range(KNOCKOUT_COUNT):
        own = jnp.where(head_ids == my_knock[k], jnp.zeros_like(own), own)
    extra = jnp.zeros_like(key3)
    for k in range(KNOCKOUT_COUNT):
        extra = jnp.where(head_ids == their_knock[k], returned[:, k : k + 1, :], extra)
    key_out = (own.astype(jnp.float32) + extra.astype(jnp.float32)).astype(jnp.bfloat16).reshape(tok_rows, -1)
    return (query_out, key_out, value_out)


def solution(mesh):
    placed = (
        P(("dp", "seq"), None),
        P(("dp", "seq"), None),
        P(("dp", "seq"), None),
        P(("dp", "seq"), None),
        P("dp", None),
        P(),
        P(),
    )
    return jax.shard_map(
        per_device,
        mesh=mesh,
        in_specs=placed,
        out_specs=(P(("dp", "seq"), None), P(("dp", "seq"), None), P(("dp", "seq"), None)),
        check_vma=False,
    )
```

```python
import math

import jax
import jax.numpy as jnp
from jax import lax
from jax.experimental import pallas as pl
from jax.experimental.pallas import tpu as pltpu
from jax.sharding import PartitionSpec as P

KEY_VALUE_HEADS = 8
HEAD_WIDTH = 128
KNOCKOUT_COUNT = 2


masked_score = -1e30


def document_mask(lengths, length):
    doc_ends = jnp.cumsum(lengths)
    position = jnp.arange(length, dtype=jnp.int32)
    segment = jnp.sum((position[:, None] >= doc_ends[None, :]).astype(jnp.int32), axis=1)
    causal = position[:, None] >= position[None, :]
    return jnp.logical_and(causal, segment[:, None] == segment[None, :])


def attend_back(query_side, key_side, value_side, grad_side, visible):
    length = query_side.shape[0]
    heads_of_query = query_side.shape[1] // HEAD_WIDTH
    scaling = 1.0 / math.sqrt(HEAD_WIDTH)

    def one_head(head_index, totals):
        query_grads, key_grads, value_gradient = totals
        query_rows = lax.dynamic_slice_in_dim(query_side, head_index * HEAD_WIDTH, HEAD_WIDTH, 1)
        grad_rows = lax.dynamic_slice_in_dim(grad_side, head_index * HEAD_WIDTH, HEAD_WIDTH, 1)
        scores = (
            jnp.einsum("id,jd->ij", query_rows, key_side, preferred_element_type=jnp.float32)
            * scaling
        )
        scores = jnp.where(visible, scores, masked_score)
        row_max = jnp.max(scores, axis=1, keepdims=True)
        weights = jnp.exp(scores - row_max)
        attn_probs = weights / jnp.sum(weights, axis=1, keepdims=True)
        probs_low = attn_probs.astype(jnp.bfloat16)
        value_part = jnp.einsum(
            "ij,id->jd", probs_low, grad_rows, preferred_element_type=jnp.float32
        )
        prob_grads = jnp.einsum(
            "id,jd->ij", grad_rows, value_side, preferred_element_type=jnp.float32
        )
        row_delta = jnp.sum(attn_probs * prob_grads, axis=1, keepdims=True)
        score_grads = (attn_probs * (prob_grads - row_delta) * scaling).astype(jnp.bfloat16)
        query_part = jnp.dot(score_grads, key_side, preferred_element_type=jnp.float32)
        key_part = jnp.einsum(
            "ij,id->jd", score_grads, query_rows, preferred_element_type=jnp.float32
        )
        query_grads = lax.dynamic_update_slice_in_dim(
            query_grads, query_part.astype(jnp.bfloat16), head_index * HEAD_WIDTH, 1
        )
        key_grads = key_grads + key_part
        value_gradient = value_gradient + value_part
        return (query_grads, key_grads, value_gradient)

    initial = (
        jnp.zeros((length, query_side.shape[1]), jnp.bfloat16),
        jnp.zeros((length, key_side.shape[1]), jnp.float32),
        jnp.zeros((length, value_side.shape[1]), jnp.float32),
    )
    return lax.fori_loop(0, heads_of_query, one_head, initial)


BLOCK_ROWS = 256


def attend_kernel(seg_row_ref, seg_col_ref, q_ref, g_ref, k_ref, v_ref, out_ref, dk_acc, dv_acc):
    scaling = 1.0 / math.sqrt(HEAD_WIDTH)
    length = q_ref.shape[0]
    head = pl.program_id(0)
    heads = pl.num_programs(0)

    @pl.when(head == 0)
    def _():
        dk_acc[...] = jnp.zeros_like(dk_acc)
        dv_acc[...] = jnp.zeros_like(dv_acc)

    dq_cols = pl.ds(pl.multiple_of(head * HEAD_WIDTH, HEAD_WIDTH), HEAD_WIDTH)
    for block in range(length // BLOCK_ROWS):
        rows = pl.ds(block * BLOCK_ROWS, BLOCK_ROWS)
        span = (block + 1) * BLOCK_ROWS
        keys = k_ref[0:span, :]
        vals = v_ref[0:span, :]
        q_rows = q_ref[rows, :]
        g_rows = g_ref[rows, :]
        scores = lax.dot_general(
            q_rows, keys, (((1,), (1,)), ((), ())), preferred_element_type=jnp.float32
        ) * scaling
        row_pos = block * BLOCK_ROWS + lax.broadcasted_iota(jnp.int32, (BLOCK_ROWS, span), 0)
        col_pos = lax.broadcasted_iota(jnp.int32, (BLOCK_ROWS, span), 1)
        same = seg_row_ref[rows, :] == seg_col_ref[:, 0:span]
        visible = jnp.logical_and(row_pos >= col_pos, same)
        scores = jnp.where(visible, scores, masked_score)
        row_max = jnp.max(scores, axis=1, keepdims=True)
        weights = jnp.exp(scores - row_max)
        probs = weights / jnp.sum(weights, axis=1, keepdims=True)
        probs_low = probs.astype(jnp.bfloat16)
        dv_acc[0:span, :] += lax.dot_general(
            probs_low, g_rows, (((0,), (0,)), ((), ())), preferred_element_type=jnp.float32
        )
        prob_grads = lax.dot_general(
            g_rows, vals, (((1,), (1,)), ((), ())), preferred_element_type=jnp.float32
        )
        row_delta = jnp.sum(probs * prob_grads, axis=1, keepdims=True)
        score_grads = (probs * (prob_grads - row_delta) * scaling).astype(jnp.bfloat16)
        out_ref[rows, dq_cols] = jnp.dot(
            score_grads, keys, preferred_element_type=jnp.float32
        ).astype(out_ref.dtype)
        dk_acc[0:span, :] += lax.dot_general(
            score_grads, q_rows, (((0,), (0,)), ((), ())), preferred_element_type=jnp.float32
        )

    @pl.when(head == heads - 1)
    def _():
        base = out_ref.shape[1] - 2 * HEAD_WIDTH
        out_ref[:, base : base + HEAD_WIDTH] = dv_acc[...].astype(out_ref.dtype)
        out_ref[:, base + HEAD_WIDTH :] = dk_acc[...].astype(out_ref.dtype)


def attend_back_kernel(gathered, segment, heads_of_query, q_block, g_block, k_block, v_block):
    length = gathered.shape[0]
    seg_row = segment.reshape(length, 1)
    seg_col = segment.reshape(1, length)
    full = lambda h: (0, 0)
    col = lambda b: pl.BlockSpec((length, HEAD_WIDTH), lambda h: (0, b))
    width = (heads_of_query + 2) * HEAD_WIDTH
    flops = 5 * 2 * length * length * HEAD_WIDTH * heads_of_query * 10 // 16
    return pl.pallas_call(
        attend_kernel,
        grid=(heads_of_query,),
        in_specs=[
            pl.BlockSpec((length, 1), full),
            pl.BlockSpec((1, length), full),
            pl.BlockSpec((length, HEAD_WIDTH), lambda h: (0, q_block + h)),
            pl.BlockSpec((length, HEAD_WIDTH), lambda h: (0, g_block + h)),
            col(k_block),
            col(v_block),
        ],
        out_specs=pl.BlockSpec((length, width), full),
        out_shape=jax.ShapeDtypeStruct((length, width), jnp.bfloat16),
        scratch_shapes=[
            pltpu.VMEM((length, HEAD_WIDTH), jnp.float32),
            pltpu.VMEM((length, HEAD_WIDTH), jnp.float32),
        ],
        compiler_params=pltpu.CompilerParams(
            dimension_semantics=("arbitrary",), vmem_limit_bytes=48 * 1024 * 1024
        ),
        cost_estimate=pl.CostEstimate(
            flops=flops,
            transcendentals=length * length * heads_of_query * 10 // 16,
            bytes_accessed=length * HEAD_WIDTH * (2 * 2 * heads_of_query + 2 * 2 + 2 * width // HEAD_WIDTH),
        ),
    )(seg_row, seg_col, gathered, gathered, gathered, gathered)

def route_block(block, order, heads):
    prompt_count = lax.axis_size("dp")
    rows = block.shape[0]
    flat = block.reshape(prompt_count, rows // prompt_count, KEY_VALUE_HEADS, HEAD_WIDTH)
    spread = lax.all_to_all(flat, "dp", 0, 0, tiled=True)
    routed = jnp.take(spread, order, axis=0)
    routed = jnp.take_along_axis(routed, heads[:, None, :, None], axis=2)
    back = lax.all_to_all(routed, "dp", 0, 0, tiled=True)
    return back.reshape(rows, KNOCKOUT_COUNT, HEAD_WIDTH)


def route(payload, order):
    prompt_count = lax.axis_size("dp")
    flat = payload.reshape(prompt_count, -1)
    spread = lax.all_to_all(flat, "dp", 0, 0, tiled=True)
    routed = jnp.take(spread, order, axis=0)
    back = lax.all_to_all(routed, "dp", 0, 0, tiled=True)
    return back.reshape(payload.shape)


def pick_heads(block, heads):
    parts = [
        lax.dynamic_slice_in_dim(block, heads[k] * HEAD_WIDTH, HEAD_WIDTH, 1)
        for k in range(KNOCKOUT_COUNT)
    ]
    return jnp.stack(parts, axis=1)


def per_device(queries, keys, values, output_gradient, seg_lengths, knocked, source):
    sequence_count = lax.axis_size("seq")
    prompt_count = lax.axis_size("dp")
    tok_rows = queries.shape[0]
    length = tok_rows * sequence_count
    prompt_index = lax.axis_index("dp")
    prompt_ids = jnp.arange(prompt_count, dtype=jnp.int32)
    consumer = jnp.zeros((prompt_count,), jnp.int32).at[source].set(prompt_ids)
    my_knock = knocked[prompt_index]
    their_knock = knocked[consumer[prompt_index]]
    head_ids = jnp.arange(KEY_VALUE_HEADS, dtype=jnp.int32)[None, :, None]

    fetched = route_block(keys, source, knocked)
    keys3 = keys.reshape(tok_rows, KEY_VALUE_HEADS, HEAD_WIDTH)
    used3 = keys3
    for k in range(KNOCKOUT_COUNT - 1, -1, -1):
        used3 = jnp.where(head_ids == my_knock[k], fetched[:, k : k + 1, :], used3)
    used_keys = used3.reshape(tok_rows, -1)

    def cols(x):
        return x.reshape(tok_rows, sequence_count, -1)

    packed = jnp.concatenate(
        [cols(queries), cols(output_gradient), cols(used_keys), cols(values)], axis=2
    )
    widths = (
        queries.shape[1] // sequence_count,
        output_gradient.shape[1] // sequence_count,
        keys.shape[1] // sequence_count,
        values.shape[1] // sequence_count,
    )
    gathered = lax.all_to_all(packed, "seq", split_axis=1, concat_axis=0, tiled=True)
    gathered = gathered.reshape(length, -1)
    offsets = [0]
    for w in widths:
        offsets.append(offsets[-1] + w)

    doc_ends = jnp.cumsum(seg_lengths[0])
    position = jnp.arange(length, dtype=jnp.int32)
    segment = jnp.sum((position[:, None] >= doc_ends[None, :]).astype(jnp.int32), axis=1)
    heads_here = widths[0] // HEAD_WIDTH
    low = attend_back_kernel(
        gathered, segment, heads_here, 0, heads_here, 2 * heads_here, 2 * heads_here + 1
    )

    low_back = lax.all_to_all(low, "seq", split_axis=0, concat_axis=1, tiled=True)
    low_back = low_back.reshape(tok_rows, sequence_count, -1)
    v_end = widths[0] + widths[3]
    query_out = low_back[:, :, : widths[0]].reshape(tok_rows, -1)
    value_out = low_back[:, :, widths[0] : v_end].reshape(tok_rows, -1)
    key_back = low_back[:, :, v_end:].reshape(tok_rows, -1)

    returning = pick_heads(key_back, my_knock)
    returned = route(returning, consumer)
    key3 = key_back.reshape(tok_rows, KEY_VALUE_HEADS, HEAD_WIDTH)
    own = key3
    for k in range(KNOCKOUT_COUNT):
        own = jnp.where(head_ids == my_knock[k], jnp.zeros_like(own), own)
    extra = jnp.zeros_like(key3)
    for k in range(KNOCKOUT_COUNT):
        extra = jnp.where(head_ids == their_knock[k], returned[:, k : k + 1, :], extra)
    key_out = (own.astype(jnp.float32) + extra.astype(jnp.float32)).astype(jnp.bfloat16).reshape(tok_rows, -1)
    return (query_out, key_out, value_out)


def solution(mesh):
    placed = (
        P(("dp", "seq"), None),
        P(("dp", "seq"), None),
        P(("dp", "seq"), None),
        P(("dp", "seq"), None),
        P("dp", None),
        P(),
        P(),
    )
    return jax.shard_map(
        per_device,
        mesh=mesh,
        in_specs=placed,
        out_specs=(P(("dp", "seq"), None), P(("dp", "seq"), None), P(("dp", "seq"), None)),
        check_vma=False,
    )
```

```python
import math

import jax
import jax.numpy as jnp
from jax import lax
from jax.experimental import pallas as pl
from jax.experimental.pallas import tpu as pltpu
from jax.sharding import PartitionSpec as P

KEY_VALUE_HEADS = 8
HEAD_WIDTH = 128
KNOCKOUT_COUNT = 2


masked_score = -1e30


def document_mask(lengths, length):
    doc_ends = jnp.cumsum(lengths)
    position = jnp.arange(length, dtype=jnp.int32)
    segment = jnp.sum((position[:, None] >= doc_ends[None, :]).astype(jnp.int32), axis=1)
    causal = position[:, None] >= position[None, :]
    return jnp.logical_and(causal, segment[:, None] == segment[None, :])


def attend_back(query_side, key_side, value_side, grad_side, visible):
    length = query_side.shape[0]
    heads_of_query = query_side.shape[1] // HEAD_WIDTH
    scaling = 1.0 / math.sqrt(HEAD_WIDTH)

    def one_head(head_index, totals):
        query_grads, key_grads, value_gradient = totals
        query_rows = lax.dynamic_slice_in_dim(query_side, head_index * HEAD_WIDTH, HEAD_WIDTH, 1)
        grad_rows = lax.dynamic_slice_in_dim(grad_side, head_index * HEAD_WIDTH, HEAD_WIDTH, 1)
        scores = (
            jnp.einsum("id,jd->ij", query_rows, key_side, preferred_element_type=jnp.float32)
            * scaling
        )
        scores = jnp.where(visible, scores, masked_score)
        row_max = jnp.max(scores, axis=1, keepdims=True)
        weights = jnp.exp(scores - row_max)
        attn_probs = weights / jnp.sum(weights, axis=1, keepdims=True)
        probs_low = attn_probs.astype(jnp.bfloat16)
        value_part = jnp.einsum(
            "ij,id->jd", probs_low, grad_rows, preferred_element_type=jnp.float32
        )
        prob_grads = jnp.einsum(
            "id,jd->ij", grad_rows, value_side, preferred_element_type=jnp.float32
        )
        row_delta = jnp.sum(attn_probs * prob_grads, axis=1, keepdims=True)
        score_grads = (attn_probs * (prob_grads - row_delta) * scaling).astype(jnp.bfloat16)
        query_part = jnp.dot(score_grads, key_side, preferred_element_type=jnp.float32)
        key_part = jnp.einsum(
            "ij,id->jd", score_grads, query_rows, preferred_element_type=jnp.float32
        )
        query_grads = lax.dynamic_update_slice_in_dim(
            query_grads, query_part.astype(jnp.bfloat16), head_index * HEAD_WIDTH, 1
        )
        key_grads = key_grads + key_part
        value_gradient = value_gradient + value_part
        return (query_grads, key_grads, value_gradient)

    initial = (
        jnp.zeros((length, query_side.shape[1]), jnp.bfloat16),
        jnp.zeros((length, key_side.shape[1]), jnp.float32),
        jnp.zeros((length, value_side.shape[1]), jnp.float32),
    )
    return lax.fori_loop(0, heads_of_query, one_head, initial)


BLOCK_ROWS = 512


def attend_kernel(seg_row_ref, seg_col_ref, q_ref, g_ref, k_ref, v_ref, dq_ref, dk_ref, dv_ref):
    scaling = 1.0 / math.sqrt(HEAD_WIDTH)
    length = q_ref.shape[0]

    @pl.when(pl.program_id(0) == 0)
    def _():
        dk_ref[...] = jnp.zeros_like(dk_ref)
        dv_ref[...] = jnp.zeros_like(dv_ref)

    for block in range(length // BLOCK_ROWS):
        rows = pl.ds(block * BLOCK_ROWS, BLOCK_ROWS)
        span = (block + 1) * BLOCK_ROWS
        keys = k_ref[0:span, :]
        vals = v_ref[0:span, :]
        q_rows = q_ref[rows, :]
        g_rows = g_ref[rows, :]
        scores = lax.dot_general(
            q_rows, keys, (((1,), (1,)), ((), ())), preferred_element_type=jnp.float32
        ) * scaling
        row_pos = block * BLOCK_ROWS + lax.broadcasted_iota(jnp.int32, (BLOCK_ROWS, span), 0)
        col_pos = lax.broadcasted_iota(jnp.int32, (BLOCK_ROWS, span), 1)
        same = seg_row_ref[rows, :] == seg_col_ref[:, 0:span]
        visible = jnp.logical_and(row_pos >= col_pos, same)
        scores = jnp.where(visible, scores, masked_score)
        row_max = jnp.max(scores, axis=1, keepdims=True)
        weights = jnp.exp(scores - row_max)
        probs = weights / jnp.sum(weights, axis=1, keepdims=True)
        probs_low = probs.astype(jnp.bfloat16)
        dv_ref[0:span, :] += lax.dot_general(
            probs_low, g_rows, (((0,), (0,)), ((), ())), preferred_element_type=jnp.float32
        )
        prob_grads = lax.dot_general(
            g_rows, vals, (((1,), (1,)), ((), ())), preferred_element_type=jnp.float32
        )
        row_delta = jnp.sum(probs * prob_grads, axis=1, keepdims=True)
        score_grads = (probs * (prob_grads - row_delta) * scaling).astype(jnp.bfloat16)
        dq_ref[rows, :] = jnp.dot(
            score_grads, keys, preferred_element_type=jnp.float32
        ).astype(dq_ref.dtype)
        dk_ref[0:span, :] += lax.dot_general(
            score_grads, q_rows, (((0,), (0,)), ((), ())), preferred_element_type=jnp.float32
        )


def attend_back_kernel(gathered, segment, heads_of_query, q_block, g_block, k_block, v_block):
    length = gathered.shape[0]
    seg_row = segment.reshape(length, 1)
    seg_col = segment.reshape(1, length)
    full = lambda h: (0, 0)
    col = lambda b: pl.BlockSpec((length, HEAD_WIDTH), lambda h: (0, b))
    flops = 5 * 2 * length * length * HEAD_WIDTH * heads_of_query * 12 // 16
    return pl.pallas_call(
        attend_kernel,
        grid=(heads_of_query,),
        in_specs=[
            pl.BlockSpec((length, 1), full),
            pl.BlockSpec((1, length), full),
            pl.BlockSpec((length, HEAD_WIDTH), lambda h: (0, q_block + h)),
            pl.BlockSpec((length, HEAD_WIDTH), lambda h: (0, g_block + h)),
            col(k_block),
            col(v_block),
        ],
        out_specs=[
            pl.BlockSpec((length, HEAD_WIDTH), lambda h: (0, h)),
            pl.BlockSpec((length, HEAD_WIDTH), full),
            pl.BlockSpec((length, HEAD_WIDTH), full),
        ],
        out_shape=[
            jax.ShapeDtypeStruct((length, heads_of_query * HEAD_WIDTH), jnp.bfloat16),
            jax.ShapeDtypeStruct((length, HEAD_WIDTH), jnp.float32),
            jax.ShapeDtypeStruct((length, HEAD_WIDTH), jnp.float32),
        ],
        compiler_params=pltpu.CompilerParams(
            dimension_semantics=("arbitrary",), vmem_limit_bytes=48 * 1024 * 1024
        ),
        cost_estimate=pl.CostEstimate(
            flops=flops,
            transcendentals=length * length * heads_of_query * 12 // 16,
            bytes_accessed=length * HEAD_WIDTH * (2 * 2 * heads_of_query + 2 * 2 + 2 * heads_of_query + 8),
        ),
    )(seg_row, seg_col, gathered, gathered, gathered, gathered)


def route_block(block, order, heads):
    prompt_count = lax.axis_size("dp")
    rows = block.shape[0]
    flat = block.reshape(prompt_count, rows // prompt_count, KEY_VALUE_HEADS, HEAD_WIDTH)
    spread = lax.all_to_all(flat, "dp", 0, 0, tiled=True)
    routed = jnp.take(spread, order, axis=0)
    routed = jnp.take_along_axis(routed, heads[:, None, :, None], axis=2)
    back = lax.all_to_all(routed, "dp", 0, 0, tiled=True)
    return back.reshape(rows, KNOCKOUT_COUNT, HEAD_WIDTH)


def route(payload, order):
    prompt_count = lax.axis_size("dp")
    flat = payload.reshape(prompt_count, -1)
    spread = lax.all_to_all(flat, "dp", 0, 0, tiled=True)
    routed = jnp.take(spread, order, axis=0)
    back = lax.all_to_all(routed, "dp", 0, 0, tiled=True)
    return back.reshape(payload.shape)


def pick_heads(block, heads):
    parts = [
        lax.dynamic_slice_in_dim(block, heads[k] * HEAD_WIDTH, HEAD_WIDTH, 1)
        for k in range(KNOCKOUT_COUNT)
    ]
    return jnp.stack(parts, axis=1)


def per_device(queries, keys, values, output_gradient, seg_lengths, knocked, source):
    sequence_count = lax.axis_size("seq")
    prompt_count = lax.axis_size("dp")
    tok_rows = queries.shape[0]
    length = tok_rows * sequence_count
    prompt_index = lax.axis_index("dp")
    prompt_ids = jnp.arange(prompt_count, dtype=jnp.int32)
    consumer = jnp.zeros((prompt_count,), jnp.int32).at[source].set(prompt_ids)
    my_knock = knocked[prompt_index]
    their_knock = knocked[consumer[prompt_index]]
    head_ids = jnp.arange(KEY_VALUE_HEADS, dtype=jnp.int32)[None, :, None]

    fetched = route_block(keys, source, knocked)
    keys3 = keys.reshape(tok_rows, KEY_VALUE_HEADS, HEAD_WIDTH)
    used3 = keys3
    for k in range(KNOCKOUT_COUNT - 1, -1, -1):
        used3 = jnp.where(head_ids == my_knock[k], fetched[:, k : k + 1, :], used3)
    used_keys = used3.reshape(tok_rows, -1)

    def cols(x):
        return x.reshape(tok_rows, sequence_count, -1)

    packed = jnp.concatenate(
        [cols(queries), cols(output_gradient), cols(used_keys), cols(values)], axis=2
    )
    widths = (
        queries.shape[1] // sequence_count,
        output_gradient.shape[1] // sequence_count,
        keys.shape[1] // sequence_count,
        values.shape[1] // sequence_count,
    )
    gathered = lax.all_to_all(packed, "seq", split_axis=1, concat_axis=0, tiled=True)
    gathered = gathered.reshape(length, -1)
    offsets = [0]
    for w in widths:
        offsets.append(offsets[-1] + w)

    doc_ends = jnp.cumsum(seg_lengths[0])
    position = jnp.arange(length, dtype=jnp.int32)
    segment = jnp.sum((position[:, None] >= doc_ends[None, :]).astype(jnp.int32), axis=1)
    heads_here = widths[0] // HEAD_WIDTH
    query_grads, key_grads, value_gradient = attend_back_kernel(
        gathered, segment, heads_here, 0, heads_here, 2 * heads_here, 2 * heads_here + 1
    )

    low = jnp.concatenate(
        [query_grads, value_gradient.astype(jnp.bfloat16), key_grads.astype(jnp.bfloat16)], axis=1
    )
    low_back = lax.all_to_all(low, "seq", split_axis=0, concat_axis=1, tiled=True)
    low_back = low_back.reshape(tok_rows, sequence_count, -1)
    v_end = widths[0] + widths[3]
    query_out = low_back[:, :, : widths[0]].reshape(tok_rows, -1)
    value_out = low_back[:, :, widths[0] : v_end].reshape(tok_rows, -1)
    key_back = low_back[:, :, v_end:].reshape(tok_rows, -1)

    returning = pick_heads(key_back, my_knock)
    returned = route(returning, consumer)
    key3 = key_back.reshape(tok_rows, KEY_VALUE_HEADS, HEAD_WIDTH)
    own = key3
    for k in range(KNOCKOUT_COUNT):
        own = jnp.where(head_ids == my_knock[k], jnp.zeros_like(own), own)
    extra = jnp.zeros_like(key3)
    for k in range(KNOCKOUT_COUNT):
        extra = jnp.where(head_ids == their_knock[k], returned[:, k : k + 1, :], extra)
    key_out = (own.astype(jnp.float32) + extra.astype(jnp.float32)).astype(jnp.bfloat16).reshape(tok_rows, -1)
    return (query_out, key_out, value_out)


def solution(mesh):
    placed = (
        P(("dp", "seq"), None),
        P(("dp", "seq"), None),
        P(("dp", "seq"), None),
        P(("dp", "seq"), None),
        P("dp", None),
        P(),
        P(),
    )
    return jax.shard_map(
        per_device,
        mesh=mesh,
        in_specs=placed,
        out_specs=(P(("dp", "seq"), None), P(("dp", "seq"), None), P(("dp", "seq"), None)),
        check_vma=False,
    )
```

```python
import math

import jax
import jax.numpy as jnp
from jax import lax
from jax.experimental import pallas as pl
from jax.experimental.pallas import tpu as pltpu
from jax.sharding import PartitionSpec as P

KEY_VALUE_HEADS = 8
HEAD_WIDTH = 128
KNOCKOUT_COUNT = 2


masked_score = -1e30


def document_mask(lengths, length):
    doc_ends = jnp.cumsum(lengths)
    position = jnp.arange(length, dtype=jnp.int32)
    segment = jnp.sum((position[:, None] >= doc_ends[None, :]).astype(jnp.int32), axis=1)
    causal = position[:, None] >= position[None, :]
    return jnp.logical_and(causal, segment[:, None] == segment[None, :])


def attend_back(query_side, key_side, value_side, grad_side, visible):
    length = query_side.shape[0]
    heads_of_query = query_side.shape[1] // HEAD_WIDTH
    scaling = 1.0 / math.sqrt(HEAD_WIDTH)

    def one_head(head_index, totals):
        query_grads, key_grads, value_gradient = totals
        query_rows = lax.dynamic_slice_in_dim(query_side, head_index * HEAD_WIDTH, HEAD_WIDTH, 1)
        grad_rows = lax.dynamic_slice_in_dim(grad_side, head_index * HEAD_WIDTH, HEAD_WIDTH, 1)
        scores = (
            jnp.einsum("id,jd->ij", query_rows, key_side, preferred_element_type=jnp.float32)
            * scaling
        )
        scores = jnp.where(visible, scores, masked_score)
        row_max = jnp.max(scores, axis=1, keepdims=True)
        weights = jnp.exp(scores - row_max)
        attn_probs = weights / jnp.sum(weights, axis=1, keepdims=True)
        probs_low = attn_probs.astype(jnp.bfloat16)
        value_part = jnp.einsum(
            "ij,id->jd", probs_low, grad_rows, preferred_element_type=jnp.float32
        )
        prob_grads = jnp.einsum(
            "id,jd->ij", grad_rows, value_side, preferred_element_type=jnp.float32
        )
        row_delta = jnp.sum(attn_probs * prob_grads, axis=1, keepdims=True)
        score_grads = (attn_probs * (prob_grads - row_delta) * scaling).astype(jnp.bfloat16)
        query_part = jnp.dot(score_grads, key_side, preferred_element_type=jnp.float32)
        key_part = jnp.einsum(
            "ij,id->jd", score_grads, query_rows, preferred_element_type=jnp.float32
        )
        query_grads = lax.dynamic_update_slice_in_dim(
            query_grads, query_part.astype(jnp.bfloat16), head_index * HEAD_WIDTH, 1
        )
        key_grads = key_grads + key_part
        value_gradient = value_gradient + value_part
        return (query_grads, key_grads, value_gradient)

    initial = (
        jnp.zeros((length, query_side.shape[1]), jnp.bfloat16),
        jnp.zeros((length, key_side.shape[1]), jnp.float32),
        jnp.zeros((length, value_side.shape[1]), jnp.float32),
    )
    return lax.fori_loop(0, heads_of_query, one_head, initial)


BLOCK_ROWS = 1024


def attend_kernel(seg_row_ref, seg_col_ref, q_ref, g_ref, k_ref, v_ref, dq_ref, dk_ref, dv_ref):
    scaling = 1.0 / math.sqrt(HEAD_WIDTH)
    length = q_ref.shape[0]

    @pl.when(pl.program_id(0) == 0)
    def _():
        dk_ref[...] = jnp.zeros_like(dk_ref)
        dv_ref[...] = jnp.zeros_like(dv_ref)

    for block in range(length // BLOCK_ROWS):
        rows = pl.ds(block * BLOCK_ROWS, BLOCK_ROWS)
        span = (block + 1) * BLOCK_ROWS
        keys = k_ref[0:span, :]
        vals = v_ref[0:span, :]
        q_rows = q_ref[rows, :]
        g_rows = g_ref[rows, :]
        scores = lax.dot_general(
            q_rows, keys, (((1,), (1,)), ((), ())), preferred_element_type=jnp.float32
        ) * scaling
        row_pos = block * BLOCK_ROWS + lax.broadcasted_iota(jnp.int32, (BLOCK_ROWS, span), 0)
        col_pos = lax.broadcasted_iota(jnp.int32, (BLOCK_ROWS, span), 1)
        same = seg_row_ref[rows, :] == seg_col_ref[:, 0:span]
        visible = jnp.logical_and(row_pos >= col_pos, same)
        scores = jnp.where(visible, scores, masked_score)
        row_max = jnp.max(scores, axis=1, keepdims=True)
        weights = jnp.exp(scores - row_max)
        probs = weights / jnp.sum(weights, axis=1, keepdims=True)
        probs_low = probs.astype(jnp.bfloat16)
        dv_ref[0:span, :] += lax.dot_general(
            probs_low, g_rows, (((0,), (0,)), ((), ())), preferred_element_type=jnp.float32
        )
        prob_grads = lax.dot_general(
            g_rows, vals, (((1,), (1,)), ((), ())), preferred_element_type=jnp.float32
        )
        row_delta = jnp.sum(probs * prob_grads, axis=1, keepdims=True)
        score_grads = (probs * (prob_grads - row_delta) * scaling).astype(jnp.bfloat16)
        dq_ref[rows, :] = jnp.dot(
            score_grads, keys, preferred_element_type=jnp.float32
        ).astype(dq_ref.dtype)
        dk_ref[0:span, :] += lax.dot_general(
            score_grads, q_rows, (((0,), (0,)), ((), ())), preferred_element_type=jnp.float32
        )


def attend_back_kernel(gathered, segment, heads_of_query, q_block, g_block, k_block, v_block):
    length = gathered.shape[0]
    seg_row = segment.reshape(length, 1)
    seg_col = segment.reshape(1, length)
    full = lambda h: (0, 0)
    col = lambda b: pl.BlockSpec((length, HEAD_WIDTH), lambda h: (0, b))
    flops = 5 * 2 * length * length * HEAD_WIDTH * heads_of_query * 16 // 16
    return pl.pallas_call(
        attend_kernel,
        grid=(heads_of_query,),
        in_specs=[
            pl.BlockSpec((length, 1), full),
            pl.BlockSpec((1, length), full),
            pl.BlockSpec((length, HEAD_WIDTH), lambda h: (0, q_block + h)),
            pl.BlockSpec((length, HEAD_WIDTH), lambda h: (0, g_block + h)),
            col(k_block),
            col(v_block),
        ],
        out_specs=[
            pl.BlockSpec((length, HEAD_WIDTH), lambda h: (0, h)),
            pl.BlockSpec((length, HEAD_WIDTH), full),
            pl.BlockSpec((length, HEAD_WIDTH), full),
        ],
        out_shape=[
            jax.ShapeDtypeStruct((length, heads_of_query * HEAD_WIDTH), jnp.bfloat16),
            jax.ShapeDtypeStruct((length, HEAD_WIDTH), jnp.float32),
            jax.ShapeDtypeStruct((length, HEAD_WIDTH), jnp.float32),
        ],
        compiler_params=pltpu.CompilerParams(
            dimension_semantics=("arbitrary",), vmem_limit_bytes=48 * 1024 * 1024
        ),
        cost_estimate=pl.CostEstimate(
            flops=flops,
            transcendentals=length * length * heads_of_query * 16 // 16,
            bytes_accessed=length * HEAD_WIDTH * (2 * 2 * heads_of_query + 2 * 2 + 2 * heads_of_query + 8),
        ),
    )(seg_row, seg_col, gathered, gathered, gathered, gathered)


def route_block(block, order, heads):
    prompt_count = lax.axis_size("dp")
    rows = block.shape[0]
    flat = block.reshape(prompt_count, rows // prompt_count, KEY_VALUE_HEADS, HEAD_WIDTH)
    spread = lax.all_to_all(flat, "dp", 0, 0, tiled=True)
    routed = jnp.take(spread, order, axis=0)
    routed = jnp.take_along_axis(routed, heads[:, None, :, None], axis=2)
    back = lax.all_to_all(routed, "dp", 0, 0, tiled=True)
    return back.reshape(rows, KNOCKOUT_COUNT, HEAD_WIDTH)


def route(payload, order):
    prompt_count = lax.axis_size("dp")
    flat = payload.reshape(prompt_count, -1)
    spread = lax.all_to_all(flat, "dp", 0, 0, tiled=True)
    routed = jnp.take(spread, order, axis=0)
    back = lax.all_to_all(routed, "dp", 0, 0, tiled=True)
    return back.reshape(payload.shape)


def pick_heads(block, heads):
    parts = [
        lax.dynamic_slice_in_dim(block, heads[k] * HEAD_WIDTH, HEAD_WIDTH, 1)
        for k in range(KNOCKOUT_COUNT)
    ]
    return jnp.stack(parts, axis=1)


def per_device(queries, keys, values, output_gradient, seg_lengths, knocked, source):
    sequence_count = lax.axis_size("seq")
    prompt_count = lax.axis_size("dp")
    tok_rows = queries.shape[0]
    length = tok_rows * sequence_count
    prompt_index = lax.axis_index("dp")
    prompt_ids = jnp.arange(prompt_count, dtype=jnp.int32)
    consumer = jnp.zeros((prompt_count,), jnp.int32).at[source].set(prompt_ids)
    my_knock = knocked[prompt_index]
    their_knock = knocked[consumer[prompt_index]]
    head_ids = jnp.arange(KEY_VALUE_HEADS, dtype=jnp.int32)[None, :, None]

    fetched = route_block(keys, source, knocked)
    keys3 = keys.reshape(tok_rows, KEY_VALUE_HEADS, HEAD_WIDTH)
    used3 = keys3
    for k in range(KNOCKOUT_COUNT - 1, -1, -1):
        used3 = jnp.where(head_ids == my_knock[k], fetched[:, k : k + 1, :], used3)
    used_keys = used3.reshape(tok_rows, -1)

    def cols(x):
        return x.reshape(tok_rows, sequence_count, -1)

    packed = jnp.concatenate(
        [cols(queries), cols(output_gradient), cols(used_keys), cols(values)], axis=2
    )
    widths = (
        queries.shape[1] // sequence_count,
        output_gradient.shape[1] // sequence_count,
        keys.shape[1] // sequence_count,
        values.shape[1] // sequence_count,
    )
    gathered = lax.all_to_all(packed, "seq", split_axis=1, concat_axis=0, tiled=True)
    gathered = gathered.reshape(length, -1)
    offsets = [0]
    for w in widths:
        offsets.append(offsets[-1] + w)

    doc_ends = jnp.cumsum(seg_lengths[0])
    position = jnp.arange(length, dtype=jnp.int32)
    segment = jnp.sum((position[:, None] >= doc_ends[None, :]).astype(jnp.int32), axis=1)
    heads_here = widths[0] // HEAD_WIDTH
    query_grads, key_grads, value_gradient = attend_back_kernel(
        gathered, segment, heads_here, 0, heads_here, 2 * heads_here, 2 * heads_here + 1
    )

    low = jnp.concatenate(
        [query_grads, value_gradient.astype(jnp.bfloat16), key_grads.astype(jnp.bfloat16)], axis=1
    )
    low_back = lax.all_to_all(low, "seq", split_axis=0, concat_axis=1, tiled=True)
    low_back = low_back.reshape(tok_rows, sequence_count, -1)
    v_end = widths[0] + widths[3]
    query_out = low_back[:, :, : widths[0]].reshape(tok_rows, -1)
    value_out = low_back[:, :, widths[0] : v_end].reshape(tok_rows, -1)
    key_back = low_back[:, :, v_end:].reshape(tok_rows, -1)

    returning = pick_heads(key_back, my_knock)
    returned = route(returning, consumer)
    key3 = key_back.reshape(tok_rows, KEY_VALUE_HEADS, HEAD_WIDTH)
    own = key3
    for k in range(KNOCKOUT_COUNT):
        own = jnp.where(head_ids == my_knock[k], jnp.zeros_like(own), own)
    extra = jnp.zeros_like(key3)
    for k in range(KNOCKOUT_COUNT):
        extra = jnp.where(head_ids == their_knock[k], returned[:, k : k + 1, :], extra)
    key_out = (own.astype(jnp.float32) + extra.astype(jnp.float32)).astype(jnp.bfloat16).reshape(tok_rows, -1)
    return (query_out, key_out, value_out)


def solution(mesh):
    placed = (
        P(("dp", "seq"), None),
        P(("dp", "seq"), None),
        P(("dp", "seq"), None),
        P(("dp", "seq"), None),
        P("dp", None),
        P(),
        P(),
    )
    return jax.shard_map(
        per_device,
        mesh=mesh,
        in_specs=placed,
        out_specs=(P(("dp", "seq"), None), P(("dp", "seq"), None), P(("dp", "seq"), None)),
        check_vma=False,
    )
```

```python
import math

import jax
import jax.numpy as jnp
from jax import lax
from jax.experimental import pallas as pl
from jax.experimental.pallas import tpu as pltpu
from jax.sharding import PartitionSpec as P

KEY_VALUE_HEADS = 8
HEAD_WIDTH = 128
KNOCKOUT_COUNT = 2


masked_score = -1e30


def document_mask(lengths, length):
    doc_ends = jnp.cumsum(lengths)
    position = jnp.arange(length, dtype=jnp.int32)
    segment = jnp.sum((position[:, None] >= doc_ends[None, :]).astype(jnp.int32), axis=1)
    causal = position[:, None] >= position[None, :]
    return jnp.logical_and(causal, segment[:, None] == segment[None, :])


def attend_back(query_side, key_side, value_side, grad_side, visible):
    length = query_side.shape[0]
    heads_of_query = query_side.shape[1] // HEAD_WIDTH
    scaling = 1.0 / math.sqrt(HEAD_WIDTH)

    def one_head(head_index, totals):
        query_grads, key_grads, value_gradient = totals
        query_rows = lax.dynamic_slice_in_dim(query_side, head_index * HEAD_WIDTH, HEAD_WIDTH, 1)
        grad_rows = lax.dynamic_slice_in_dim(grad_side, head_index * HEAD_WIDTH, HEAD_WIDTH, 1)
        scores = (
            jnp.einsum("id,jd->ij", query_rows, key_side, preferred_element_type=jnp.float32)
            * scaling
        )
        scores = jnp.where(visible, scores, masked_score)
        row_max = jnp.max(scores, axis=1, keepdims=True)
        weights = jnp.exp(scores - row_max)
        attn_probs = weights / jnp.sum(weights, axis=1, keepdims=True)
        probs_low = attn_probs.astype(jnp.bfloat16)
        value_part = jnp.einsum(
            "ij,id->jd", probs_low, grad_rows, preferred_element_type=jnp.float32
        )
        prob_grads = jnp.einsum(
            "id,jd->ij", grad_rows, value_side, preferred_element_type=jnp.float32
        )
        row_delta = jnp.sum(attn_probs * prob_grads, axis=1, keepdims=True)
        score_grads = (attn_probs * (prob_grads - row_delta) * scaling).astype(jnp.bfloat16)
        query_part = jnp.dot(score_grads, key_side, preferred_element_type=jnp.float32)
        key_part = jnp.einsum(
            "ij,id->jd", score_grads, query_rows, preferred_element_type=jnp.float32
        )
        query_grads = lax.dynamic_update_slice_in_dim(
            query_grads, query_part.astype(jnp.bfloat16), head_index * HEAD_WIDTH, 1
        )
        key_grads = key_grads + key_part
        value_gradient = value_gradient + value_part
        return (query_grads, key_grads, value_gradient)

    initial = (
        jnp.zeros((length, query_side.shape[1]), jnp.bfloat16),
        jnp.zeros((length, key_side.shape[1]), jnp.float32),
        jnp.zeros((length, value_side.shape[1]), jnp.float32),
    )
    return lax.fori_loop(0, heads_of_query, one_head, initial)


BLOCK_ROWS = 512


def attend_kernel(seg_row_ref, seg_col_ref, q_ref, g_ref, k_ref, v_ref, dq_ref, dk_ref, dv_ref):
    scaling = 1.0 / math.sqrt(HEAD_WIDTH)
    length = q_ref.shape[0]

    @pl.when(pl.program_id(0) == 0)
    def _():
        dk_ref[...] = jnp.zeros_like(dk_ref)
        dv_ref[...] = jnp.zeros_like(dv_ref)

    bounds = [0, 3 * length // 8, 3 * length // 4, length]
    for block in range(len(bounds) - 1):
        first, size = bounds[block], bounds[block + 1] - bounds[block]
        rows = pl.ds(first, size)
        span = bounds[block + 1]
        keys = k_ref[0:span, :]
        vals = v_ref[0:span, :]
        q_rows = q_ref[rows, :]
        g_rows = g_ref[rows, :]
        scores = lax.dot_general(
            q_rows, keys, (((1,), (1,)), ((), ())), preferred_element_type=jnp.float32
        ) * scaling
        row_pos = first + lax.broadcasted_iota(jnp.int32, (size, span), 0)
        col_pos = lax.broadcasted_iota(jnp.int32, (size, span), 1)
        same = seg_row_ref[rows, :] == seg_col_ref[:, 0:span]
        visible = jnp.logical_and(row_pos >= col_pos, same)
        scores = jnp.where(visible, scores, masked_score)
        row_max = jnp.max(scores, axis=1, keepdims=True)
        weights = jnp.exp(scores - row_max)
        probs = weights / jnp.sum(weights, axis=1, keepdims=True)
        probs_low = probs.astype(jnp.bfloat16)
        dv_ref[0:span, :] += lax.dot_general(
            probs_low, g_rows, (((0,), (0,)), ((), ())), preferred_element_type=jnp.float32
        )
        prob_grads = lax.dot_general(
            g_rows, vals, (((1,), (1,)), ((), ())), preferred_element_type=jnp.float32
        )
        row_delta = jnp.sum(probs * prob_grads, axis=1, keepdims=True)
        score_grads = (probs * (prob_grads - row_delta) * scaling).astype(jnp.bfloat16)
        dq_ref[rows, :] = jnp.dot(
            score_grads, keys, preferred_element_type=jnp.float32
        ).astype(dq_ref.dtype)
        dk_ref[0:span, :] += lax.dot_general(
            score_grads, q_rows, (((0,), (0,)), ((), ())), preferred_element_type=jnp.float32
        )


def attend_back_kernel(gathered, segment, heads_of_query, q_block, g_block, k_block, v_block):
    length = gathered.shape[0]
    seg_row = segment.reshape(length, 1)
    seg_col = segment.reshape(1, length)
    full = lambda h: (0, 0)
    col = lambda b: pl.BlockSpec((length, HEAD_WIDTH), lambda h: (0, b))
    flops = 5 * 2 * length * length * HEAD_WIDTH * heads_of_query * 11 // 16
    return pl.pallas_call(
        attend_kernel,
        grid=(heads_of_query,),
        in_specs=[
            pl.BlockSpec((length, 1), full),
            pl.BlockSpec((1, length), full),
            pl.BlockSpec((length, HEAD_WIDTH), lambda h: (0, q_block + h)),
            pl.BlockSpec((length, HEAD_WIDTH), lambda h: (0, g_block + h)),
            col(k_block),
            col(v_block),
        ],
        out_specs=[
            pl.BlockSpec((length, HEAD_WIDTH), lambda h: (0, h)),
            pl.BlockSpec((length, HEAD_WIDTH), full),
            pl.BlockSpec((length, HEAD_WIDTH), full),
        ],
        out_shape=[
            jax.ShapeDtypeStruct((length, heads_of_query * HEAD_WIDTH), jnp.bfloat16),
            jax.ShapeDtypeStruct((length, HEAD_WIDTH), jnp.float32),
            jax.ShapeDtypeStruct((length, HEAD_WIDTH), jnp.float32),
        ],
        compiler_params=pltpu.CompilerParams(
            dimension_semantics=("arbitrary",), vmem_limit_bytes=48 * 1024 * 1024
        ),
        cost_estimate=pl.CostEstimate(
            flops=flops,
            transcendentals=length * length * heads_of_query * 11 // 16,
            bytes_accessed=length * HEAD_WIDTH * (2 * 2 * heads_of_query + 2 * 2 + 2 * heads_of_query + 8),
        ),
    )(seg_row, seg_col, gathered, gathered, gathered, gathered)


def route_block(block, order, heads):
    prompt_count = lax.axis_size("dp")
    rows = block.shape[0]
    flat = block.reshape(prompt_count, rows // prompt_count, KEY_VALUE_HEADS, HEAD_WIDTH)
    spread = lax.all_to_all(flat, "dp", 0, 0, tiled=True)
    routed = jnp.take(spread, order, axis=0)
    routed = jnp.take_along_axis(routed, heads[:, None, :, None], axis=2)
    back = lax.all_to_all(routed, "dp", 0, 0, tiled=True)
    return back.reshape(rows, KNOCKOUT_COUNT, HEAD_WIDTH)


def route(payload, order):
    prompt_count = lax.axis_size("dp")
    flat = payload.reshape(prompt_count, -1)
    spread = lax.all_to_all(flat, "dp", 0, 0, tiled=True)
    routed = jnp.take(spread, order, axis=0)
    back = lax.all_to_all(routed, "dp", 0, 0, tiled=True)
    return back.reshape(payload.shape)


def pick_heads(block, heads):
    parts = [
        lax.dynamic_slice_in_dim(block, heads[k] * HEAD_WIDTH, HEAD_WIDTH, 1)
        for k in range(KNOCKOUT_COUNT)
    ]
    return jnp.stack(parts, axis=1)


def per_device(queries, keys, values, output_gradient, seg_lengths, knocked, source):
    sequence_count = lax.axis_size("seq")
    prompt_count = lax.axis_size("dp")
    tok_rows = queries.shape[0]
    length = tok_rows * sequence_count
    prompt_index = lax.axis_index("dp")
    prompt_ids = jnp.arange(prompt_count, dtype=jnp.int32)
    consumer = jnp.zeros((prompt_count,), jnp.int32).at[source].set(prompt_ids)
    my_knock = knocked[prompt_index]
    their_knock = knocked[consumer[prompt_index]]
    head_ids = jnp.arange(KEY_VALUE_HEADS, dtype=jnp.int32)[None, :, None]

    fetched = route_block(keys, source, knocked)
    keys3 = keys.reshape(tok_rows, KEY_VALUE_HEADS, HEAD_WIDTH)
    used3 = keys3
    for k in range(KNOCKOUT_COUNT - 1, -1, -1):
        used3 = jnp.where(head_ids == my_knock[k], fetched[:, k : k + 1, :], used3)
    used_keys = used3.reshape(tok_rows, -1)

    def cols(x):
        return x.reshape(tok_rows, sequence_count, -1)

    packed = jnp.concatenate(
        [cols(queries), cols(output_gradient), cols(used_keys), cols(values)], axis=2
    )
    widths = (
        queries.shape[1] // sequence_count,
        output_gradient.shape[1] // sequence_count,
        keys.shape[1] // sequence_count,
        values.shape[1] // sequence_count,
    )
    gathered = lax.all_to_all(packed, "seq", split_axis=1, concat_axis=0, tiled=True)
    gathered = gathered.reshape(length, -1)
    offsets = [0]
    for w in widths:
        offsets.append(offsets[-1] + w)

    doc_ends = jnp.cumsum(seg_lengths[0])
    position = jnp.arange(length, dtype=jnp.int32)
    segment = jnp.sum((position[:, None] >= doc_ends[None, :]).astype(jnp.int32), axis=1)
    heads_here = widths[0] // HEAD_WIDTH
    query_grads, key_grads, value_gradient = attend_back_kernel(
        gathered, segment, heads_here, 0, heads_here, 2 * heads_here, 2 * heads_here + 1
    )

    low = jnp.concatenate(
        [query_grads, value_gradient.astype(jnp.bfloat16), key_grads.astype(jnp.bfloat16)], axis=1
    )
    low_back = lax.all_to_all(low, "seq", split_axis=0, concat_axis=1, tiled=True)
    low_back = low_back.reshape(tok_rows, sequence_count, -1)
    v_end = widths[0] + widths[3]
    query_out = low_back[:, :, : widths[0]].reshape(tok_rows, -1)
    value_out = low_back[:, :, widths[0] : v_end].reshape(tok_rows, -1)
    key_back = low_back[:, :, v_end:].reshape(tok_rows, -1)

    returning = pick_heads(key_back, my_knock)
    returned = route(returning, consumer)
    key3 = key_back.reshape(tok_rows, KEY_VALUE_HEADS, HEAD_WIDTH)
    own = key3
    for k in range(KNOCKOUT_COUNT):
        own = jnp.where(head_ids == my_knock[k], jnp.zeros_like(own), own)
    extra = jnp.zeros_like(key3)
    for k in range(KNOCKOUT_COUNT):
        extra = jnp.where(head_ids == their_knock[k], returned[:, k : k + 1, :], extra)
    key_out = (own.astype(jnp.float32) + extra.astype(jnp.float32)).astype(jnp.bfloat16).reshape(tok_rows, -1)
    return (query_out, key_out, value_out)


def solution(mesh):
    placed = (
        P(("dp", "seq"), None),
        P(("dp", "seq"), None),
        P(("dp", "seq"), None),
        P(("dp", "seq"), None),
        P("dp", None),
        P(),
        P(),
    )
    return jax.shard_map(
        per_device,
        mesh=mesh,
        in_specs=placed,
        out_specs=(P(("dp", "seq"), None), P(("dp", "seq"), None), P(("dp", "seq"), None)),
        check_vma=False,
    )
```
